512 devices in a mesh: ctx: 16 (over z), ep: 32 (over x, y, core).
Axes of the slice: x: 4, y: 4, z: 16, core: 2. Of those that a mesh axis runs over, the one named last changes fastest.
Arguments:
- queries: bfloat16 [4096, 8192], P('ctx', 'ep'), may hold values from -6 to 6
- key_rows: bfloat16 [4096, 8192], P('ctx', 'ep'), may hold values from -6 to 6
- value_rows: bfloat16 [4096, 8192], P('ctx', 'ep'), may hold values from -6 to 6
- log_decay: float32 [4096, 64], P('ctx', 'ep'), may hold values from -1 to 0
- out_weight: bfloat16 [6144, 8192], P('ep'), may hold values from -0.0625 to 0.0625
- expert_ids: int32 [4096, 2], P('ctx'), may hold values from 0 to 31, all different within a row; in each aligned block of 256 rows (0 to 255, 256 to 511, ...) at most 32 rows name the same one
- flagged: int32 [1024], P('ctx'), may hold values from 0 to 4095, as said below
- direction: float32 [6144], P('ep'), as said below
Outputs:
- expert_tiles: bfloat16 [32, 512, 6144], P('ep', 'ctx')
The draws below stay inside these ranges and needn't reach their ends.
Inputs may be any that keep to these rules, and one draw needn't show every extreme that they name: `expert_ids`: each row names 2 different experts; among the 256 rows of one block of the sequence no expert is named more than 32 times, a bound that some block reaches. `flagged`: entries 64 * b to 64 * b + 63 are distinct rows of block b of 256 rows. `direction`: not all zero.
All inputs are finite; a program needn't handle non-finite values.
Results may differ from the reference program's by a relative error of at most 0.0059.
Values may be sent and summed in bfloat16 or wider, within the bound.
No kernel may reach another device: no remote copies, remote signals or barrier semaphores. Data moves between devices by JAX's collectives and lax.ppermute only.
A program may use at most 64 MiB of HBM per device.

```python
import math
import jax
import jax.numpy as jnp
import numpy as np
from jax import lax

MODEL = 6144
HEAD_COUNT = 64
HEAD = 128
TOP = 2
SUB = 256
ROWS_PER_BLOCK = 256
FLAG_DEV = 64
EXPERTS = 32
SEQUENCE_LENGTH = 4096
CAP = 32
N_CTX = 16


def draw_log_decay(key, part):
    key_sequence = jax.random.split(key, 6)
    head_pick = jax.random.uniform(key_sequence[0], (HEAD_COUNT,))
    fast_share = 0.5
    quick_decay_heads = head_pick < fast_share
    fast_rate = math.log(10.0) / (30.0 + 20.0 * jax.random.uniform(key_sequence[1], (HEAD_COUNT,)))
    slow_rate = math.log(2.0) / SEQUENCE_LENGTH
    base_rate = jnp.where(quick_decay_heads, fast_rate, slow_rate)
    every_block = SEQUENCE_LENGTH // ROWS_PER_BLOCK
    low_end = -math.log(2.0)
    high_end = math.log(2.0)
    block_factor = jnp.exp(jax.random.uniform(key_sequence[2], (every_block, 1, HEAD_COUNT), minval=low_end, maxval=high_end))
    position_factor = jnp.exp(jax.random.uniform(key_sequence[3], (every_block, ROWS_PER_BLOCK, HEAD_COUNT), minval=low_end, maxval=high_end))
    rate_all = base_rate[None, None, :] * block_factor * position_factor
    spike_events = jax.random.uniform(key_sequence[4], (every_block, ROWS_PER_BLOCK, HEAD_COUNT)) < 3.0 / SEQUENCE_LENGTH
    spike_falloff = jnp.log(jax.random.uniform(key_sequence[5], (every_block, ROWS_PER_BLOCK, HEAD_COUNT), minval=0.5, maxval=0.8))
    skipped_ahead = jnp.where(spike_events & jnp.logical_not(quick_decay_heads)[None, None, :], spike_falloff, 0.0)
    return (skipped_ahead - rate_all).reshape(SEQUENCE_LENGTH, HEAD_COUNT).astype(jnp.float32)


def draw_flagged(key, part):
    every_block = SEQUENCE_LENGTH // ROWS_PER_BLOCK
    key_sequence = jax.random.split(key, every_block)

    def choose_rows(block_key):
        order = jax.random.permutation(block_key, ROWS_PER_BLOCK).astype(jnp.int32)
        return ((order - order[0]) % ROWS_PER_BLOCK)[:FLAG_DEV]
    chosen = jax.vmap(choose_rows)(key_sequence).astype(jnp.int32)
    block_index = jnp.arange(every_block, dtype=jnp.int32)[:, None]
    mirrored = jnp.where(block_index % 2 == 1, ROWS_PER_BLOCK - 1 - chosen, chosen)
    starts = block_index * ROWS_PER_BLOCK
    return (mirrored + starts).reshape(-1).astype(jnp.int32)


def draw_direction(key, part):
    key_sequence = jax.random.split(key, 2)
    width = MODEL
    magnitude = jnp.exp(jax.random.uniform(key_sequence[0], (width,)) * math.log(64.0))
    signed = jax.random.normal(key_sequence[1], (width,))
    return (signed * magnitude / 16.0).astype(jnp.float32)


def levels(own_key, dims, cuts, low, high):
    gain = 1.0
    for position, parts in cuts:
        steps = jax.random.uniform(jax.random.fold_in(jax.random.fold_in(own_key, 6), position), (parts,), jnp.float32, low / len(cuts), high / len(cuts))
        gain = gain * jnp.repeat(jnp.exp(steps), dims[position] // parts).reshape((-1,) + (1,) * (len(dims) - 1 - position))
    return gain


def routed_block(own_key, own, number, rows, amount, top, most, skew):
    sequence = jax.random.permutation(own_key, amount)
    heavy_load, common = portions_of(amount, rows * top, most, skew, True), portions_of(amount, rows * top, most, skew, False)
    places = jnp.arange(amount)

    def named(tallies, offset_by):
        used = int((tallies > 0).sum())
        fixed = max(1, used // 4)
        shifted = fixed + (places - fixed + offset_by * (used - fixed)) % max(1, amount - fixed)
        return jnp.zeros((amount,), jnp.int32).at[sequence[jnp.where(places < fixed, places, shifted)]].set(jnp.asarray(tallies, jnp.int32))

    tallies = jnp.where(number % 4 == 0, named(heavy_load, number // 4), named(common, number - number // 4 - 1))
    mixed = jax.random.permutation(jax.random.fold_in(own, 3), amount)
    source_of, receiver = mixed[0:amount // 2 * 2:2], mixed[1:amount // 2 * 2:2]
    room = jnp.minimum(tallies[source_of] - 1, most - tallies[receiver]) // 2
    room = jnp.where((source_of == sequence[0]) | (receiver == sequence[0]) | (tallies[receiver] == 0), 0, jnp.maximum(room, 0))
    shifted = jax.random.randint(jax.random.fold_in(own, 4), (amount // 2,), 0, 1 << 20) % (room + 1)
    tallies = tallies.at[source_of].add(-shifted).at[receiver].add(shifted)
    labels = jnp.searchsorted(jnp.cumsum(tallies), jnp.arange(rows * top), side="right").astype(jnp.int32)
    listing = labels.reshape(top, rows).T
    listing = listing[jax.random.permutation(jax.random.fold_in(own, 1), rows)]
    offset_by = jax.random.randint(jax.random.fold_in(own, 2), (rows, 1), 0, top)
    return jnp.take_along_axis(listing, (jnp.arange(top)[None, :] + offset_by) % top, axis=1)


def portions_of(amount, total, limit, skew, full):
    loads = [(1 << 20) // math.isqrt(standing ** skew) + 1 for standing in range(1, amount + 1)]
    largest = limit if full else min(limit, max(-(-total // amount), total * loads[0] // sum(loads)))
    least = 1 if total - largest >= amount - 1 else 0
    given, spare = [largest] + [least] * (amount - 1), total - largest - least * (amount - 1)
    while spare > 0:
        candidates = [i for i in range(1, amount) if given[i] < largest] or [i for i in range(1, amount) if given[i] < limit]
        pool, remaining = sum([loads[i] for i in candidates]), spare
        for i in candidates:
            addition = min(limit - given[i], max(1, remaining * loads[i] // pool), spare)
            given[i] = given[i] + addition
            spare = spare - addition
    return np.array(given)


def bell_draw(key, dims, deviation, reach, cuts=(), kind=jnp.bfloat16):
    result = deviation * jax.random.normal(key, dims, jnp.float32)
    if cuts:
        result = result * levels(key, dims, cuts, -0.22, 0.18)
    return jnp.clip(result, -reach, reach).astype(kind)


def setup_inputs(seed: int = 0) -> dict:
    streams_of = jax.random.split(jax.random.key(seed), 9)
    queries = bell_draw(streams_of[0], (SEQUENCE_LENGTH, HEAD_COUNT * HEAD), 1.0, 6.0, ((0, 16), (1, 32)))
    key_rows = bell_draw(streams_of[1], (SEQUENCE_LENGTH, HEAD_COUNT * HEAD), 1.0, 6.0, ((0, 16), (1, 32)))
    value_rows = bell_draw(streams_of[2], (SEQUENCE_LENGTH, HEAD_COUNT * HEAD), 1.0, 6.0, ((0, 16), (1, 32)))
    log_decay = draw_log_decay(jax.random.fold_in(streams_of[8], 71), 0)
    out_weight = bell_draw(streams_of[4], (MODEL, HEAD_COUNT * HEAD), (HEAD_COUNT * HEAD) ** -0.5, 0.0625, ((0, 32),))
    expert_ids_keys = jax.random.split(jax.random.fold_in(streams_of[5], 1), SEQUENCE_LENGTH // ROWS_PER_BLOCK)
    expert_ids_turns = jax.random.permutation(jax.random.fold_in(streams_of[5], 3), SEQUENCE_LENGTH // ROWS_PER_BLOCK)
    expert_ids = jax.vmap(lambda own, number: routed_block(jax.random.fold_in(streams_of[5], 2), own, number, ROWS_PER_BLOCK, EXPERTS, TOP, CAP, 1))(expert_ids_keys, expert_ids_turns).reshape((SEQUENCE_LENGTH, TOP))
    flagged = draw_flagged(jax.random.fold_in(streams_of[8], 71), 0)
    direction = draw_direction(jax.random.fold_in(streams_of[8], 71), 0)
    return dict(queries=queries, key_rows=key_rows, value_rows=value_rows, log_decay=log_decay, out_weight=out_weight, expert_ids=expert_ids, flagged=flagged, direction=direction)


def sub_step(kv_state, pieces):
    query_sub, key_sub, value_sub, decay_sub = pieces
    cumulated = jnp.cumsum(decay_sub, axis=0)
    scores = jnp.einsum('thd,shd->hts', query_sub.astype(jnp.float32), key_sub.astype(jnp.float32))
    spread = jnp.transpose(cumulated)
    decay_gaps = jnp.minimum(spread[:, :, None] - spread[:, None, :], 0.0)
    causal = jnp.arange(SUB, dtype=jnp.int32)[:, None] >= jnp.arange(SUB, dtype=jnp.int32)[None, :]
    weights = jnp.where(causal[None], scores * jnp.exp(decay_gaps), 0.0).astype(jnp.bfloat16)
    inside = jnp.einsum('hts,shd->thd', weights.astype(jnp.float32), value_sub.astype(jnp.float32))
    scaled = query_sub.astype(jnp.float32) * jnp.exp(cumulated)[:, :, None]
    carried = jnp.einsum('thd,hde->the', scaled, kv_state, precision=lax.Precision.HIGHEST)
    last_decay = cumulated[-1]
    key_scaled = (key_sub.astype(jnp.float32) * jnp.exp(last_decay[None, :] - cumulated)[:, :, None]).astype(jnp.bfloat16)
    update = jnp.einsum('shd,she->hde', key_scaled.astype(jnp.float32), value_sub.astype(jnp.float32))
    kv_state = jnp.exp(last_decay)[:, None, None] * kv_state + update
    return (kv_state, inside + carried)

def normalize(outputs):
    mean_square = lax.optimization_barrier(jnp.mean(outputs * outputs, axis=-1, keepdims=True))
    return (outputs * lax.rsqrt(mean_square + 1e-06)).astype(jnp.bfloat16)

def reference(queries, key_rows, value_rows, log_decay, out_weight, expert_ids, flagged, direction):
    sub_count = SEQUENCE_LENGTH // SUB

    def shaped(operand):
        return operand.reshape(sub_count, SUB, HEAD_COUNT, HEAD)
    start_state = jnp.zeros((HEAD_COUNT, HEAD, HEAD), jnp.float32)
    final_state, outputs = lax.scan(sub_step, start_state, (shaped(queries), shaped(key_rows), shaped(value_rows), log_decay.reshape(sub_count, SUB, HEAD_COUNT)))
    attended = normalize(outputs).reshape(SEQUENCE_LENGTH, HEAD_COUNT * HEAD)
    projected = lax.dot_general(attended, out_weight, (((1,), (1,)), ((), ())), preferred_element_type=jnp.float32).astype(jnp.bfloat16)
    norm_square = jnp.sum(direction * direction) + 1e-06
    picked = projected[flagged].astype(jnp.float32)
    products = jnp.dot(picked, direction, precision=lax.Precision.HIGHEST)
    removed = (picked - (products / norm_square)[:, None] * direction[None, :]).astype(jnp.bfloat16)
    ablated = projected.at[flagged].set(removed)
    grouped = expert_ids.reshape(N_CTX, ROWS_PER_BLOCK * TOP)
    matches = (grouped[:, :, None] == jnp.arange(EXPERTS, dtype=jnp.int32)[None, None, :]).astype(jnp.int32)
    slot_index = lax.optimization_barrier(jnp.sum((jnp.cumsum(matches, axis=1) - matches) * matches, axis=2)).reshape(-1)
    source = jnp.arange(SEQUENCE_LENGTH * TOP, dtype=jnp.int32) // TOP
    positions = source // ROWS_PER_BLOCK * CAP + slot_index
    tile_rows = jnp.zeros((EXPERTS, N_CTX * CAP, MODEL), jnp.bfloat16)
    return tile_rows.at[expert_ids.reshape(-1), positions].set(ablated[source])
```

```python
import jax
import jax.numpy as jnp
from jax import lax
from jax.sharding import PartitionSpec as P

HEAD = 128
TOP = 2
EXP_DEV = 1
SUB = 256
PAD_ROWS = 8
PARTS = 3


def local_step(carried_in, pieces):
    kv_state, offset = carried_in
    query_sub, key_sub, value_sub, decay_sub = pieces
    sub_rows = query_sub.shape[0]
    cumulated = jnp.cumsum(decay_sub, axis=0)
    scores = jnp.einsum("thd,shd->hts", query_sub, key_sub, preferred_element_type=jnp.float32)
    spread = jnp.transpose(cumulated)
    decay_gaps = jnp.minimum(spread[:, :, None] - spread[:, None, :], 0.0)
    causal = (
        jnp.arange(sub_rows, dtype=jnp.int32)[:, None]
        >= jnp.arange(sub_rows, dtype=jnp.int32)[None, :]
    )
    weights = jnp.where(causal[None], scores * jnp.exp(decay_gaps), 0.0).astype(jnp.bfloat16)
    inside = jnp.einsum("hts,shd->thd", weights, value_sub, preferred_element_type=jnp.float32)
    scaled = query_sub.astype(jnp.float32) * jnp.exp(cumulated)[:, :, None]
    carried = jnp.einsum("thd,hde->the", scaled, kv_state, precision=lax.Precision.HIGHEST)
    last_decay = cumulated[-1]
    key_scaled = (
        key_sub.astype(jnp.float32) * jnp.exp(last_decay[None, :] - cumulated)[:, :, None]
    ).astype(jnp.bfloat16)
    update = jnp.einsum("shd,she->hde", key_scaled, value_sub, preferred_element_type=jnp.float32)
    kv_state = jnp.exp(last_decay)[:, None, None] * kv_state + update
    reach_decay = jnp.exp(offset[None, :] + cumulated)
    return ((kv_state, offset + last_decay), (inside + carried, reach_decay))


def normalize(outputs):
    mean_square = jnp.mean(outputs * outputs, axis=-1, keepdims=True)
    return (outputs * lax.rsqrt(mean_square + 1e-06)).astype(jnp.bfloat16)


def split_parts(values, width):
    pieces = []
    rest = values
    for _ in range(PARTS):
        part = lax.reduce_precision(rest, exponent_bits=8, mantissa_bits=7)
        pieces.append(part)
        rest = rest - part
    stacked = jnp.stack(pieces).astype(jnp.bfloat16)
    return jnp.pad(stacked, ((0, PAD_ROWS - PARTS), (0, width - values.shape[0])))


def joined_parts(rows, width, used):
    pieces = rows.astype(jnp.float32).reshape(PARTS, -1, width)[:, :, :used].reshape(PARTS, -1)
    total = pieces[0]
    for part in range(1, PARTS):
        total = total + pieces[part]
    return total


def local(queries, key_rows, value_rows, log_decay, out_weight, expert_ids, flagged, direction):
    block_rows = queries.shape[0]
    local_width = queries.shape[1]
    local_heads = local_width // HEAD
    sub_count = block_rows // SUB
    model_cols = out_weight.shape[0]
    ctx_count = lax.axis_size("ctx")
    ctx_index = lax.axis_index("ctx")
    ep_index = lax.axis_index("ep")

    def shaped(operand):
        return operand.reshape(sub_count, SUB, local_heads, HEAD)

    start_state = (
        jnp.zeros((local_heads, HEAD, HEAD), jnp.float32),
        jnp.zeros((local_heads,), jnp.float32),
    )
    scanned = lax.scan(
        local_step,
        start_state,
        (
            shaped(queries),
            shaped(key_rows),
            shaped(value_rows),
            log_decay.reshape(sub_count, SUB, local_heads),
        ),
    )
    local_state, total_decay = scanned[0]
    partial_out, reach_decay = scanned[1]

    packed = jnp.concatenate(
        [local_state, jnp.broadcast_to(total_decay[:, None, None], (local_heads, PAD_ROWS, HEAD))],
        axis=1,
    )
    gathered = lax.all_gather(packed, "ctx", axis=0)
    states = gathered[:, :, :HEAD, :]
    gains = jnp.exp(gathered[:, :, HEAD, 0])
    incoming = jnp.zeros_like(local_state)
    for source in range(ctx_count - 1):
        folded = gains[source][:, None, None] * incoming + states[source]
        incoming = jnp.where(source < ctx_index, folded, incoming)

    scaled = shaped(queries).astype(jnp.float32) * reach_decay[..., None]
    outputs = partial_out + jnp.einsum(
        "cthd,hde->cthe", scaled, incoming, precision=lax.Precision.HIGHEST
    )
    attended = normalize(outputs).reshape(block_rows, local_width)
    riders = split_parts(direction, local_width)
    gathered_rows = lax.all_gather(
        jnp.concatenate([attended, riders], axis=0), "ep", axis=1, tiled=True
    )
    projected = lax.dot_general(
        gathered_rows,
        out_weight,
        (((1,), (1,)), ((), ())),
        preferred_element_type=jnp.float32,
    ).astype(jnp.bfloat16)[:block_rows]
    direction_full = joined_parts(gathered_rows[block_rows : block_rows + PARTS], local_width, model_cols)

    experts_all = lax.axis_size("ep") * EXP_DEV
    capacity = 2 * block_rows * TOP // experts_all
    flat_ids = expert_ids.reshape(-1)
    matches = (flat_ids[:, None] == jnp.arange(experts_all, dtype=jnp.int32)[None, :]).astype(
        jnp.int32
    )
    slot_index = jnp.sum((jnp.cumsum(matches, axis=0) - matches) * matches, axis=1)
    position = (flat_ids * capacity + slot_index).reshape(block_rows, TOP)
    places = jnp.arange(experts_all * capacity, dtype=jnp.int32)[:, None]
    chosen = (position[None, :, 0] == places) | (position[None, :, 1] == places)
    for pick in range(2, TOP):
        chosen = chosen | (position[None, :, pick] == places)
    tile_rows = jnp.dot(
        chosen.astype(jnp.bfloat16), projected, preferred_element_type=jnp.float32
    ).astype(jnp.bfloat16)
    tile_rows = tile_rows.reshape(experts_all, capacity, model_cols)
    received = lax.all_to_all(tile_rows, "ep", split_axis=0, concat_axis=2, tiled=True)

    local_flags = flagged - ctx_index * block_rows
    token_flag = jnp.any(
        local_flags[None, :] == jnp.arange(block_rows, dtype=jnp.int32)[:, None], axis=1
    )
    source = jnp.arange(block_rows * TOP, dtype=jnp.int32) // TOP
    owned = (flat_ids // EXP_DEV == ep_index) & token_flag[source]
    slot_ids = (flat_ids % EXP_DEV) * capacity + slot_index
    slot_flag = jnp.any(
        owned[None, :]
        & (slot_ids[None, :] == jnp.arange(EXP_DEV * capacity, dtype=jnp.int32)[:, None]),
        axis=1,
    ).reshape(EXP_DEV, capacity)

    norm_square = jnp.sum(direction_full * direction_full) + 1e-06
    rows = received.astype(jnp.float32)
    products = jnp.einsum("ecm,m->ec", rows, direction_full, precision=lax.Precision.HIGHEST)
    removed = (
        rows - (products / norm_square)[:, :, None] * direction_full[None, None, :]
    ).astype(jnp.bfloat16)
    return jnp.where(slot_flag[:, :, None], removed, received)


def solution(mesh):
    placed = (
        P("ctx", "ep"),
        P("ctx", "ep"),
        P("ctx", "ep"),
        P("ctx", "ep"),
        P("ep", None),
        P("ctx", None),
        P("ctx"),
        P("ep"),
    )
    return jax.shard_map(
        local, mesh=mesh, in_specs=placed, out_specs=P("ep", "ctx", None), check_vma=False
    )
```

```python
import jax
import jax.numpy as jnp
from jax import lax
from jax.sharding import PartitionSpec as P

HEAD = 128
TOP = 2
EXP_DEV = 1
SUB = 256
PAD_ROWS = 8
PARTS = 3


def local_step(carried_in, pieces):
    kv_state, offset = carried_in
    query_sub, key_sub, value_sub, decay_sub = pieces
    sub_rows = query_sub.shape[0]
    cumulated = jnp.cumsum(decay_sub, axis=0)
    scores = jnp.einsum("thd,shd->hts", query_sub, key_sub, preferred_element_type=jnp.float32)
    spread = jnp.transpose(cumulated)
    decay_gaps = jnp.minimum(spread[:, :, None] - spread[:, None, :], 0.0)
    causal = (
        jnp.arange(sub_rows, dtype=jnp.int32)[:, None]
        >= jnp.arange(sub_rows, dtype=jnp.int32)[None, :]
    )
    weights = jnp.where(causal[None], scores * jnp.exp(decay_gaps), 0.0).astype(jnp.bfloat16)
    inside = jnp.einsum("hts,shd->thd", weights, value_sub, preferred_element_type=jnp.float32)
    scaled = query_sub.astype(jnp.float32) * jnp.exp(cumulated)[:, :, None]
    carried = jnp.einsum("thd,hde->the", scaled, kv_state, precision=lax.Precision.HIGHEST)
    last_decay = cumulated[-1]
    key_scaled = (
        key_sub.astype(jnp.float32) * jnp.exp(last_decay[None, :] - cumulated)[:, :, None]
    ).astype(jnp.bfloat16)
    update = jnp.einsum("shd,she->hde", key_scaled, value_sub, preferred_element_type=jnp.float32)
    kv_state = jnp.exp(last_decay)[:, None, None] * kv_state + update
    reach_decay = jnp.exp(offset[None, :] + cumulated)
    return ((kv_state, offset + last_decay), (inside + carried, reach_decay))


def normalize(outputs):
    mean_square = jnp.mean(outputs * outputs, axis=-1, keepdims=True)
    return (outputs * lax.rsqrt(mean_square + 1e-06)).astype(jnp.bfloat16)


def passed_along(value, axis, steps):
    count = lax.axis_size(axis)
    return lax.ppermute(value, axis, [(source, source + steps) for source in range(count - steps)])


def combined(left, right):
    right_log = right[:, HEAD:, :]
    gain = jnp.exp(right_log[:, :1, :1])
    state = gain * left[:, :HEAD, :] + right[:, :HEAD, :]
    return jnp.concatenate([state, right_log + left[:, HEAD:, :]], axis=1)


def split_parts(values, width):
    pieces = []
    rest = values
    for _ in range(PARTS):
        part = lax.reduce_precision(rest, exponent_bits=8, mantissa_bits=7)
        pieces.append(part)
        rest = rest - part
    stacked = jnp.stack(pieces).astype(jnp.bfloat16)
    return jnp.pad(stacked, ((0, PAD_ROWS - PARTS), (0, width - values.shape[0])))


def joined_parts(rows, width, used):
    pieces = rows.astype(jnp.float32).reshape(PARTS, -1, width)[:, :, :used].reshape(PARTS, -1)
    total = pieces[0]
    for part in range(1, PARTS):
        total = total + pieces[part]
    return total


def local(queries, key_rows, value_rows, log_decay, out_weight, expert_ids, flagged, direction):
    block_rows = queries.shape[0]
    local_width = queries.shape[1]
    local_heads = local_width // HEAD
    sub_count = block_rows // SUB
    model_cols = out_weight.shape[0]
    ctx_count = lax.axis_size("ctx")
    ctx_index = lax.axis_index("ctx")
    ep_index = lax.axis_index("ep")

    def shaped(operand):
        return operand.reshape(sub_count, SUB, local_heads, HEAD)

    start_state = (
        jnp.zeros((local_heads, HEAD, HEAD), jnp.float32),
        jnp.zeros((local_heads,), jnp.float32),
    )
    scanned = lax.scan(
        local_step,
        start_state,
        (
            shaped(queries),
            shaped(key_rows),
            shaped(value_rows),
            log_decay.reshape(sub_count, SUB, local_heads),
        ),
    )
    local_state, total_decay = scanned[0]
    partial_out, reach_decay = scanned[1]

    packed = jnp.concatenate(
        [local_state, jnp.broadcast_to(total_decay[:, None, None], (local_heads, PAD_ROWS, HEAD))],
        axis=1,
    )
    inclusive = packed
    exclusive = None
    distance = 1
    while distance < ctx_count:
        arrived = passed_along(inclusive, "ctx", distance)
        exclusive = arrived if exclusive is None else combined(arrived, exclusive)
        if 2 * distance < ctx_count:
            inclusive = combined(arrived, inclusive)
        distance *= 2
    incoming = (
        jnp.zeros_like(local_state) if exclusive is None else exclusive[:, :HEAD, :]
    )

    scaled = shaped(queries).astype(jnp.float32) * reach_decay[..., None]
    outputs = partial_out + jnp.einsum(
        "cthd,hde->cthe", scaled, incoming, precision=lax.Precision.HIGHEST
    )
    attended = normalize(outputs).reshape(block_rows, local_width)
    riders = split_parts(direction, local_width)
    gathered_rows = lax.all_gather(
        jnp.concatenate([attended, riders], axis=0), "ep", axis=1, tiled=True
    )
    projected = lax.dot_general(
        gathered_rows,
        out_weight,
        (((1,), (1,)), ((), ())),
        preferred_element_type=jnp.float32,
    ).astype(jnp.bfloat16)[:block_rows]
    direction_full = joined_parts(gathered_rows[block_rows : block_rows + PARTS], local_width, model_cols)

    experts_all = lax.axis_size("ep") * EXP_DEV
    capacity = 2 * block_rows * TOP // experts_all
    flat_ids = expert_ids.reshape(-1)
    matches = (flat_ids[:, None] == jnp.arange(experts_all, dtype=jnp.int32)[None, :]).astype(
        jnp.int32
    )
    slot_index = jnp.sum((jnp.cumsum(matches, axis=0) - matches) * matches, axis=1)
    position = (flat_ids * capacity + slot_index).reshape(block_rows, TOP)
    places = jnp.arange(experts_all * capacity, dtype=jnp.int32)[:, None]
    chosen = (position[None, :, 0] == places) | (position[None, :, 1] == places)
    for pick in range(2, TOP):
        chosen = chosen | (position[None, :, pick] == places)
    tile_rows = jnp.dot(
        chosen.astype(jnp.bfloat16), projected, preferred_element_type=jnp.float32
    ).astype(jnp.bfloat16)
    tile_rows = tile_rows.reshape(experts_all, capacity, model_cols)
    received = lax.all_to_all(tile_rows, "ep", split_axis=0, concat_axis=2, tiled=True)

    local_flags = flagged - ctx_index * block_rows
    token_flag = jnp.any(
        local_flags[None, :] == jnp.arange(block_rows, dtype=jnp.int32)[:, None], axis=1
    )
    source = jnp.arange(block_rows * TOP, dtype=jnp.int32) // TOP
    owned = (flat_ids // EXP_DEV == ep_index) & token_flag[source]
    slot_ids = (flat_ids % EXP_DEV) * capacity + slot_index
    slot_flag = jnp.any(
        owned[None, :]
        & (slot_ids[None, :] == jnp.arange(EXP_DEV * capacity, dtype=jnp.int32)[:, None]),
        axis=1,
    ).reshape(EXP_DEV, capacity)

    norm_square = jnp.sum(direction_full * direction_full) + 1e-06
    rows = received.astype(jnp.float32)
    products = jnp.einsum("ecm,m->ec", rows, direction_full, precision=lax.Precision.HIGHEST)
    removed = (
        rows - (products / norm_square)[:, :, None] * direction_full[None, None, :]
    ).astype(jnp.bfloat16)
    return jnp.where(slot_flag[:, :, None], removed, received)


def solution(mesh):
    placed = (
        P("ctx", "ep"),
        P("ctx", "ep"),
        P("ctx", "ep"),
        P("ctx", "ep"),
        P("ep", None),
        P("ctx", None),
        P("ctx"),
        P("ep"),
    )
    return jax.shard_map(
        local, mesh=mesh, in_specs=placed, out_specs=P("ep", "ctx", None), check_vma=False
    )
```

```python
import jax
import jax.numpy as jnp
import numpy as np
from jax import lax
from jax.sharding import Mesh
from jax.sharding import PartitionSpec as P

HEAD = 128
TOP = 2
EXP_DEV = 1
SUB = 256
PAD_ROWS = 8
PARTS = 3
RING = 4
EP = ("x", "y", "core")
OFFSETS = (0, -1, 1, 2)


def local_step(carried_in, pieces):
    kv_state, offset = carried_in
    query_sub, key_sub, value_sub, decay_sub = pieces
    sub_rows = query_sub.shape[0]
    cumulated = jnp.cumsum(decay_sub, axis=0)
    scores = jnp.einsum("thd,shd->hts", query_sub, key_sub, preferred_element_type=jnp.float32)
    spread = jnp.transpose(cumulated)
    decay_gaps = jnp.minimum(spread[:, :, None] - spread[:, None, :], 0.0)
    causal = (
        jnp.arange(sub_rows, dtype=jnp.int32)[:, None]
        >= jnp.arange(sub_rows, dtype=jnp.int32)[None, :]
    )
    weights = jnp.where(causal[None], scores * jnp.exp(decay_gaps), 0.0).astype(jnp.bfloat16)
    inside = jnp.einsum("hts,shd->thd", weights, value_sub, preferred_element_type=jnp.float32)
    scaled = query_sub.astype(jnp.float32) * jnp.exp(cumulated)[:, :, None]
    carried = jnp.einsum("thd,hde->the", scaled, kv_state, precision=lax.Precision.HIGHEST)
    last_decay = cumulated[-1]
    key_scaled = (
        key_sub.astype(jnp.float32) * jnp.exp(last_decay[None, :] - cumulated)[:, :, None]
    ).astype(jnp.bfloat16)
    update = jnp.einsum("shd,she->hde", key_scaled, value_sub, preferred_element_type=jnp.float32)
    kv_state = jnp.exp(last_decay)[:, None, None] * kv_state + update
    reach_decay = jnp.exp(offset[None, :] + cumulated)
    return ((kv_state, offset + last_decay), (inside + carried, reach_decay))


def normalize(outputs):
    mean_square = jnp.mean(outputs * outputs, axis=-1, keepdims=True)
    return (outputs * lax.rsqrt(mean_square + 1e-06)).astype(jnp.bfloat16)


def passed_along(value, axis, steps):
    count = lax.axis_size(axis)
    return lax.ppermute(value, axis, [(source, source + steps) for source in range(count - steps)])


def combined(left, right):
    right_log = right[:, HEAD:, :]
    gain = jnp.exp(right_log[:, :1, :1])
    state = gain * left[:, :HEAD, :] + right[:, :HEAD, :]
    return jnp.concatenate([state, right_log + left[:, HEAD:, :]], axis=1)


def ring_gathered(blocks, axis):
    forward = [(i, (i + 1) % RING) for i in range(RING)]
    backward = [(i, (i - 1) % RING) for i in range(RING)]
    half = blocks.shape[-1] // 2
    from_left = lax.ppermute(blocks, axis, forward)
    from_right = lax.ppermute(blocks, axis, backward)
    far_left = lax.ppermute(from_left[..., :half], axis, forward)
    far_right = lax.ppermute(from_right[..., half:], axis, backward)
    far = jnp.concatenate([far_left, far_right], axis=-1)
    return jnp.concatenate([blocks, from_left, from_right, far], axis=0)


def split_parts(values, width):
    pieces = []
    rest = values
    for _ in range(PARTS):
        part = lax.reduce_precision(rest, exponent_bits=8, mantissa_bits=7)
        pieces.append(part)
        rest = rest - part
    stacked = jnp.stack(pieces).astype(jnp.bfloat16)
    return jnp.pad(stacked, ((0, PAD_ROWS - PARTS), (0, width - values.shape[0])))


def joined_parts(rows, width, used):
    pieces = rows.astype(jnp.float32).reshape(PARTS, -1, width)[:, :, :used].reshape(PARTS, -1)
    total = pieces[0]
    for part in range(1, PARTS):
        total = total + pieces[part]
    return total


def local(queries, key_rows, value_rows, log_decay, out_weight, expert_ids, flagged, direction):
    block_rows = queries.shape[0]
    local_width = queries.shape[1]
    local_heads = local_width // HEAD
    sub_count = block_rows // SUB
    model_cols = out_weight.shape[0]
    ctx_count = lax.axis_size("ctx")
    ctx_index = lax.axis_index("ctx")
    ep_index = lax.axis_index(EP)

    def shaped(operand):
        return operand.reshape(sub_count, SUB, local_heads, HEAD)

    start_state = (
        jnp.zeros((local_heads, HEAD, HEAD), jnp.float32),
        jnp.zeros((local_heads,), jnp.float32),
    )
    scanned = lax.scan(
        local_step,
        start_state,
        (
            shaped(queries),
            shaped(key_rows),
            shaped(value_rows),
            log_decay.reshape(sub_count, SUB, local_heads),
        ),
    )
    local_state, total_decay = scanned[0]
    partial_out, reach_decay = scanned[1]

    packed = jnp.concatenate(
        [local_state, jnp.broadcast_to(total_decay[:, None, None], (local_heads, PAD_ROWS, HEAD))],
        axis=1,
    )
    inclusive = packed
    exclusive = None
    distance = 1
    while distance < ctx_count:
        arrived = passed_along(inclusive, "ctx", distance)
        exclusive = arrived if exclusive is None else combined(arrived, exclusive)
        if 2 * distance < ctx_count:
            inclusive = combined(arrived, inclusive)
        distance *= 2
    incoming = (
        jnp.zeros_like(local_state) if exclusive is None else exclusive[:, :HEAD, :]
    )

    scaled = shaped(queries).astype(jnp.float32) * reach_decay[..., None]
    outputs = partial_out + jnp.einsum(
        "cthd,hde->cthe", scaled, incoming, precision=lax.Precision.HIGHEST
    )
    attended = normalize(outputs).reshape(block_rows, local_width)
    riders = split_parts(direction, local_width)
    block = jnp.concatenate([attended, riders], axis=0)
    near = ring_gathered(ring_gathered(block[None], "x"), "y")
    far = lax.ppermute(near, "core", [(0, 1), (1, 0)])

    offsets = jnp.asarray(OFFSETS, jnp.int32)
    origin_x = (lax.axis_index("x") + offsets) % RING
    origin_y = (lax.axis_index("y") + offsets) % RING
    near_origin = ((origin_x[None, :] * RING + origin_y[:, None]) * 2).reshape(-1)
    core_index = lax.axis_index("core")
    origin = jnp.concatenate([near_origin + core_index, near_origin + (1 - core_index)])
    slots = origin.shape[0]
    weight_slots = jnp.take(out_weight.reshape(model_cols, slots, local_width), origin, axis=1)
    half = near.shape[0]
    projected = lax.dot_general(
        near,
        weight_slots[:, :half],
        (((0, 2), (1, 2)), ((), ())),
        preferred_element_type=jnp.float32,
    ) + lax.dot_general(
        far,
        weight_slots[:, half:],
        (((0, 2), (1, 2)), ((), ())),
        preferred_element_type=jnp.float32,
    )
    projected = projected.astype(jnp.bfloat16)[:block_rows]
    rider_rows = jnp.concatenate(
        [near[:, block_rows : block_rows + PARTS], far[:, block_rows : block_rows + PARTS]], axis=0
    )
    reorder = (origin[None, :] == jnp.arange(slots, dtype=jnp.int32)[:, None]).astype(jnp.bfloat16)
    ordered = jnp.einsum("os,spk->pok", reorder, rider_rows, preferred_element_type=jnp.float32)
    direction_full = joined_parts(ordered.astype(jnp.bfloat16), local_width, model_cols)

    experts_all = lax.axis_size(EP) * EXP_DEV
    capacity = 2 * block_rows * TOP // experts_all
    flat_ids = expert_ids.reshape(-1)
    matches = (flat_ids[:, None] == jnp.arange(experts_all, dtype=jnp.int32)[None, :]).astype(
        jnp.int32
    )
    slot_index = jnp.sum((jnp.cumsum(matches, axis=0) - matches) * matches, axis=1)
    position = (flat_ids * capacity + slot_index).reshape(block_rows, TOP)
    places = jnp.arange(experts_all * capacity, dtype=jnp.int32)[:, None]
    chosen = (position[None, :, 0] == places) | (position[None, :, 1] == places)
    for pick in range(2, TOP):
        chosen = chosen | (position[None, :, pick] == places)
    tile_rows = jnp.dot(
        chosen.astype(jnp.bfloat16), projected, preferred_element_type=jnp.float32
    ).astype(jnp.bfloat16)
    tile_rows = tile_rows.reshape(experts_all, capacity, model_cols)
    received = lax.all_to_all(tile_rows, EP, split_axis=0, concat_axis=2, tiled=True)

    local_flags = flagged - ctx_index * block_rows
    token_flag = jnp.any(
        local_flags[None, :] == jnp.arange(block_rows, dtype=jnp.int32)[:, None], axis=1
    )
    source = jnp.arange(block_rows * TOP, dtype=jnp.int32) // TOP
    owned = (flat_ids // EXP_DEV == ep_index) & token_flag[source]
    slot_ids = (flat_ids % EXP_DEV) * capacity + slot_index
    slot_flag = jnp.any(
        owned[None, :]
        & (slot_ids[None, :] == jnp.arange(EXP_DEV * capacity, dtype=jnp.int32)[:, None]),
        axis=1,
    ).reshape(EXP_DEV, capacity)

    norm_square = jnp.sum(direction_full * direction_full) + 1e-06
    rows = received.astype(jnp.float32)
    products = jnp.einsum("ecm,m->ec", rows, direction_full, precision=lax.Precision.HIGHEST)
    removed = (
        rows - (products / norm_square)[:, :, None] * direction_full[None, None, :]
    ).astype(jnp.bfloat16)
    return jnp.where(slot_flag[:, :, None], removed, received)


def solution(mesh):
    devices = np.asarray(mesh.devices)
    fine = Mesh(devices.reshape(devices.shape[0], RING, RING, 2), ("ctx",) + EP)
    placed = (
        P("ctx", EP),
        P("ctx", EP),
        P("ctx", EP),
        P("ctx", EP),
        P(EP, None),
        P("ctx", None),
        P("ctx"),
        P(EP),
    )
    return jax.shard_map(
        local, mesh=fine, in_specs=placed, out_specs=P(EP, "ctx", None), check_vma=False
    )
```

```python
import jax
import jax.numpy as jnp
import numpy as np
from jax import lax
from jax.sharding import Mesh
from jax.sharding import PartitionSpec as P

HEAD = 128
TOP = 2
EXP_DEV = 1
SUB = 256
PAD_ROWS = 8
PARTS = 3
RING = 4
EP = ("x", "y", "core")


def local_step(carried_in, pieces):
    kv_state, offset = carried_in
    query_sub, key_sub, value_sub, decay_sub = pieces
    sub_rows = query_sub.shape[0]
    cumulated = jnp.cumsum(decay_sub, axis=0)
    scores = jnp.einsum("thd,shd->hts", query_sub, key_sub, preferred_element_type=jnp.float32)
    spread = jnp.transpose(cumulated)
    decay_gaps = jnp.minimum(spread[:, :, None] - spread[:, None, :], 0.0)
    causal = (
        jnp.arange(sub_rows, dtype=jnp.int32)[:, None]
        >= jnp.arange(sub_rows, dtype=jnp.int32)[None, :]
    )
    weights = jnp.where(causal[None], scores * jnp.exp(decay_gaps), 0.0).astype(jnp.bfloat16)
    inside = jnp.einsum("hts,shd->thd", weights, value_sub, preferred_element_type=jnp.float32)
    scaled = query_sub.astype(jnp.float32) * jnp.exp(cumulated)[:, :, None]
    carried = jnp.einsum("thd,hde->the", scaled, kv_state, precision=lax.Precision.HIGHEST)
    last_decay = cumulated[-1]
    key_scaled = (
        key_sub.astype(jnp.float32) * jnp.exp(last_decay[None, :] - cumulated)[:, :, None]
    ).astype(jnp.bfloat16)
    update = jnp.einsum("shd,she->hde", key_scaled, value_sub, preferred_element_type=jnp.float32)
    kv_state = jnp.exp(last_decay)[:, None, None] * kv_state + update
    reach_decay = jnp.exp(offset[None, :] + cumulated)
    return ((kv_state, offset + last_decay), (inside + carried, reach_decay))


def normalize(outputs):
    mean_square = jnp.mean(outputs * outputs, axis=-1, keepdims=True)
    return (outputs * lax.rsqrt(mean_square + 1e-06)).astype(jnp.bfloat16)


def passed_along(value, axis, steps):
    count = lax.axis_size(axis)
    return lax.ppermute(value, axis, [(source, source + steps) for source in range(count - steps)])


def combined(left, right):
    right_log = right[:, HEAD:, :]
    gain = jnp.exp(right_log[:, :1, :1])
    state = gain * left[:, :HEAD, :] + right[:, :HEAD, :]
    return jnp.concatenate([state, right_log + left[:, HEAD:, :]], axis=1)


def ring_gathered(blocks, axis):
    def shifted(value, steps):
        return lax.ppermute(value, axis, [(i, (i + steps) % RING) for i in range(RING)])

    half = blocks.shape[-1] // 2
    from_right = shifted(blocks, -1)
    from_left = shifted(blocks, 1)
    far = jnp.concatenate([shifted(blocks[..., :half], 2), shifted(blocks[..., half:], -2)], axis=-1)
    return jnp.concatenate([blocks, from_right, far, from_left], axis=0)


def split_parts(values, width):
    pieces = []
    rest = values
    for _ in range(PARTS):
        part = lax.reduce_precision(rest, exponent_bits=8, mantissa_bits=7)
        pieces.append(part)
        rest = rest - part
    stacked = jnp.stack(pieces).astype(jnp.bfloat16)
    return jnp.pad(stacked, ((0, PAD_ROWS - PARTS), (0, width - values.shape[0])))


def joined_parts(rows, width, used):
    pieces = rows.astype(jnp.float32).reshape(PARTS, -1, width)[:, :, :used].reshape(PARTS, -1)
    total = pieces[0]
    for part in range(1, PARTS):
        total = total + pieces[part]
    return total


def local(queries, key_rows, value_rows, log_decay, out_weight, expert_ids, flagged, direction):
    block_rows = queries.shape[0]
    local_width = queries.shape[1]
    local_heads = local_width // HEAD
    sub_count = block_rows // SUB
    model_cols = out_weight.shape[0]
    ctx_count = lax.axis_size("ctx")
    ctx_index = lax.axis_index("ctx")
    ep_index = lax.axis_index(EP)

    def shaped(operand):
        return operand.reshape(sub_count, SUB, local_heads, HEAD)

    start_state = (
        jnp.zeros((local_heads, HEAD, HEAD), jnp.float32),
        jnp.zeros((local_heads,), jnp.float32),
    )
    scanned = lax.scan(
        local_step,
        start_state,
        (
            shaped(queries),
            shaped(key_rows),
            shaped(value_rows),
            log_decay.reshape(sub_count, SUB, local_heads),
        ),
    )
    local_state, total_decay = scanned[0]
    partial_out, reach_decay = scanned[1]

    packed = jnp.concatenate(
        [local_state, jnp.broadcast_to(total_decay[:, None, None], (local_heads, PAD_ROWS, HEAD))],
        axis=1,
    )
    inclusive = packed
    exclusive = None
    distance = 1
    while distance < ctx_count:
        arrived = passed_along(inclusive, "ctx", distance)
        exclusive = arrived if exclusive is None else combined(arrived, exclusive)
        if 2 * distance < ctx_count:
            inclusive = combined(arrived, inclusive)
        distance *= 2
    incoming = (
        jnp.zeros_like(local_state) if exclusive is None else exclusive[:, :HEAD, :]
    )

    scaled = shaped(queries).astype(jnp.float32) * reach_decay[..., None]
    outputs = partial_out + jnp.einsum(
        "cthd,hde->cthe", scaled, incoming, precision=lax.Precision.HIGHEST
    )
    attended = normalize(outputs).reshape(block_rows, local_width)
    riders = split_parts(direction, local_width)
    block = jnp.concatenate([attended, riders], axis=0)
    near = ring_gathered(ring_gathered(block[None], "x"), "y")
    far = lax.ppermute(near, "core", [(0, 1), (1, 0)])

    offsets = jnp.arange(RING, dtype=jnp.int32)
    origin_x = (lax.axis_index("x") + offsets) % RING
    origin_y = (lax.axis_index("y") + offsets) % RING
    near_origin = ((origin_x[None, :] * RING + origin_y[:, None]) * 2).reshape(-1)
    core_index = lax.axis_index("core")
    origin = jnp.concatenate([near_origin + core_index, near_origin + (1 - core_index)])
    slots = origin.shape[0]
    weight_slots = jnp.take(
        out_weight.reshape(model_cols, slots, local_width), origin, axis=1, mode="clip"
    )
    half = near.shape[0]
    projected = lax.dot_general(
        near,
        weight_slots[:, :half],
        (((0, 2), (1, 2)), ((), ())),
        preferred_element_type=jnp.float32,
    ) + lax.dot_general(
        far,
        weight_slots[:, half:],
        (((0, 2), (1, 2)), ((), ())),
        preferred_element_type=jnp.float32,
    )
    projected = projected.astype(jnp.bfloat16)[:block_rows]
    rider_rows = jnp.concatenate(
        [near[:, block_rows : block_rows + PARTS], far[:, block_rows : block_rows + PARTS]], axis=0
    )
    reorder = (origin[None, :] == jnp.arange(slots, dtype=jnp.int32)[:, None]).astype(jnp.bfloat16)
    ordered = jnp.einsum("os,spk->pok", reorder, rider_rows, preferred_element_type=jnp.float32)
    direction_full = joined_parts(ordered.astype(jnp.bfloat16), local_width, model_cols)

    experts_all = lax.axis_size(EP) * EXP_DEV
    capacity = 2 * block_rows * TOP // experts_all
    flat_ids = expert_ids.reshape(-1)
    matches = (flat_ids[:, None] == jnp.arange(experts_all, dtype=jnp.int32)[None, :]).astype(
        jnp.int32
    )
    slot_index = jnp.sum((jnp.cumsum(matches, axis=0) - matches) * matches, axis=1)
    position = (flat_ids * capacity + slot_index).reshape(block_rows, TOP)
    places = jnp.arange(experts_all * capacity, dtype=jnp.int32)[:, None]
    chosen = (position[None, :, 0] == places) | (position[None, :, 1] == places)
    for pick in range(2, TOP):
        chosen = chosen | (position[None, :, pick] == places)
    tile_rows = jnp.dot(
        chosen.astype(jnp.bfloat16), projected, preferred_element_type=jnp.float32
    ).astype(jnp.bfloat16)
    tile_rows = tile_rows.reshape(experts_all, capacity, model_cols)
    received = lax.all_to_all(tile_rows, EP, split_axis=0, concat_axis=2, tiled=True)

    local_flags = flagged - ctx_index * block_rows
    token_flag = jnp.any(
        local_flags[None, :] == jnp.arange(block_rows, dtype=jnp.int32)[:, None], axis=1
    )
    owned = ((expert_ids // EXP_DEV == ep_index) & token_flag[:, None]).reshape(-1)
    slot_ids = (flat_ids % EXP_DEV) * capacity + slot_index
    slot_flag = jnp.any(
        owned[None, :]
        & (slot_ids[None, :] == jnp.arange(EXP_DEV * capacity, dtype=jnp.int32)[:, None]),
        axis=1,
    ).reshape(EXP_DEV, capacity)

    norm_square = jnp.sum(direction_full * direction_full) + 1e-06
    rows = received.astype(jnp.float32)
    products = jnp.einsum("ecm,m->ec", rows, direction_full, precision=lax.Precision.HIGHEST)
    removed = (
        rows - (products / norm_square)[:, :, None] * direction_full[None, None, :]
    ).astype(jnp.bfloat16)
    return jnp.where(slot_flag[:, :, None], removed, received)


def solution(mesh):
    devices = np.asarray(mesh.devices)
    fine = Mesh(devices.reshape(devices.shape[0], RING, RING, 2), ("ctx",) + EP)
    placed = (
        P("ctx", EP),
        P("ctx", EP),
        P("ctx", EP),
        P("ctx", EP),
        P(EP, None),
        P("ctx", None),
        P("ctx"),
        P(EP),
    )
    return jax.shard_map(
        local, mesh=fine, in_specs=placed, out_specs=P(EP, "ctx", None), check_vma=False
    )
```

```python
import jax
import jax.numpy as jnp
import numpy as np
from jax import lax
from jax.sharding import Mesh
from jax.sharding import PartitionSpec as P

HEAD = 128
TOP = 2
EXP_DEV = 1
SUB = 256
PAD_ROWS = 8
PARTS = 3
RING = 4
EP = ("x", "y", "core")


def local_step(carried_in, pieces):
    kv_state, offset = carried_in
    query_sub, key_sub, value_sub, decay_sub = pieces
    sub_rows = query_sub.shape[0]
    cumulated = jnp.cumsum(decay_sub, axis=0)
    scores = jnp.einsum("thd,shd->hts", query_sub, key_sub, preferred_element_type=jnp.float32)
    spread = jnp.transpose(cumulated)
    decay_gaps = jnp.minimum(spread[:, :, None] - spread[:, None, :], 0.0)
    causal = (
        jnp.arange(sub_rows, dtype=jnp.int32)[:, None]
        >= jnp.arange(sub_rows, dtype=jnp.int32)[None, :]
    )
    weights = jnp.where(causal[None], scores * jnp.exp(decay_gaps), 0.0).astype(jnp.bfloat16)
    inside = jnp.einsum("hts,shd->thd", weights, value_sub, preferred_element_type=jnp.float32)
    scaled = query_sub.astype(jnp.float32) * jnp.exp(cumulated)[:, :, None]
    carried = jnp.einsum("thd,hde->the", scaled, kv_state, precision=lax.Precision.HIGHEST)
    last_decay = cumulated[-1]
    key_scaled = (
        key_sub.astype(jnp.float32) * jnp.exp(last_decay[None, :] - cumulated)[:, :, None]
    ).astype(jnp.bfloat16)
    update = jnp.einsum("shd,she->hde", key_scaled, value_sub, preferred_element_type=jnp.float32)
    kv_state = jnp.exp(last_decay)[:, None, None] * kv_state + update
    reach_decay = jnp.exp(offset[None, :] + cumulated)
    return ((kv_state, offset + last_decay), (inside + carried, reach_decay))


def normalize(outputs):
    mean_square = jnp.mean(outputs * outputs, axis=-1, keepdims=True)
    return (outputs * lax.rsqrt(mean_square + 1e-06)).astype(jnp.bfloat16)


def passed_along(value, axis, steps):
    count = lax.axis_size(axis)
    return lax.ppermute(value, axis, [(source, source + steps) for source in range(count - steps)])


def combined(left, right):
    right_log = right[:, HEAD:, :]
    gain = jnp.exp(right_log[:, :1, :1])
    state = gain * left[:, :HEAD, :] + right[:, :HEAD, :]
    return jnp.concatenate([state, right_log + left[:, HEAD:, :]], axis=1)


def ring_gathered(blocks, axis):
    def shifted(value, steps):
        return lax.ppermute(value, axis, [(i, (i + steps) % RING) for i in range(RING)])

    half = blocks.shape[-1] // 2
    from_right = shifted(blocks, -1)
    from_left = shifted(blocks, 1)
    far = jnp.concatenate([shifted(blocks[..., :half], 2), shifted(blocks[..., half:], -2)], axis=-1)
    return jnp.concatenate([blocks, from_right, far, from_left], axis=0)


def received_by(pairs, count, position):
    table = [False] * count
    for _, target in pairs:
        table[target] = True
    return jnp.asarray(table)[position]


def exclusive_scan(value, axis, count):
    position = lax.axis_index(axis)
    if count == 1:
        return jnp.zeros_like(value)

    def step(current, pairs, merge):
        arrived = lax.ppermute(current, axis, pairs)
        return arrived, jnp.where(received_by(pairs, count, position), merge(arrived), current)

    segment = value
    left_raw = None
    distance = 1
    while 4 * distance <= count:
        pairs = [(j - distance, j) for j in range(count) if (j + 1) % (2 * distance) == 0]
        arrived, segment = step(segment, pairs, lambda got, seg=segment: combined(got, seg))
        if left_raw is None:
            left_raw = arrived
        distance *= 2
    distance //= 2
    while distance >= 2:
        pairs = [
            (j, j + distance)
            for j in range(count)
            if (j + 1) % (2 * distance) == 0 and j + distance < count
        ]
        _, segment = step(segment, pairs, lambda got, seg=segment: combined(got, seg))
        distance //= 2
    if left_raw is None:
        left_raw = lax.ppermute(segment, axis, [(j - 1, j) for j in range(1, count, 2)])
    to_even = [(j, j + 1) for j in range(1, count - 1, 2)]
    to_odd = [(j, j + 2) for j in range(1, count - 2, 2)]
    from_odd = lax.ppermute(segment, axis, to_even)
    from_odd_far = lax.ppermute(segment, axis, to_odd)
    odd_result = jnp.where(position >= 3, combined(from_odd_far, left_raw), left_raw)
    result = jnp.where(position % 2 == 1, odd_result, from_odd)
    return jnp.where(position == 0, jnp.zeros_like(value), result)


def split_parts(values, width):
    pieces = []
    rest = values
    for _ in range(PARTS):
        part = lax.reduce_precision(rest, exponent_bits=8, mantissa_bits=7)
        pieces.append(part)
        rest = rest - part
    stacked = jnp.stack(pieces).astype(jnp.bfloat16)
    return jnp.pad(stacked, ((0, PAD_ROWS - PARTS), (0, width - values.shape[0])))


def joined_parts(rows, width, used):
    pieces = rows.astype(jnp.float32).reshape(PARTS, -1, width)[:, :, :used].reshape(PARTS, -1)
    total = pieces[0]
    for part in range(1, PARTS):
        total = total + pieces[part]
    return total


def local(queries, key_rows, value_rows, log_decay, out_weight, expert_ids, flagged, direction):
    block_rows = queries.shape[0]
    local_width = queries.shape[1]
    local_heads = local_width // HEAD
    sub_count = block_rows // SUB
    model_cols = out_weight.shape[0]
    ctx_count = lax.axis_size("ctx")
    ctx_index = lax.axis_index("ctx")
    ep_index = lax.axis_index(EP)

    def shaped(operand):
        return operand.reshape(sub_count, SUB, local_heads, HEAD)

    start_state = (
        jnp.zeros((local_heads, HEAD, HEAD), jnp.float32),
        jnp.zeros((local_heads,), jnp.float32),
    )
    scanned = lax.scan(
        local_step,
        start_state,
        (
            shaped(queries),
            shaped(key_rows),
            shaped(value_rows),
            log_decay.reshape(sub_count, SUB, local_heads),
        ),
    )
    local_state, total_decay = scanned[0]
    partial_out, reach_decay = scanned[1]

    packed = jnp.concatenate(
        [local_state, jnp.broadcast_to(total_decay[:, None, None], (local_heads, PAD_ROWS, HEAD))],
        axis=1,
    )
    exclusive = exclusive_scan(packed, "ctx", ctx_count)
    incoming = exclusive[:, :HEAD, :]

    scaled = shaped(queries).astype(jnp.float32) * reach_decay[..., None]
    outputs = partial_out + jnp.einsum(
        "cthd,hde->cthe", scaled, incoming, precision=lax.Precision.HIGHEST
    )
    attended = normalize(outputs).reshape(block_rows, local_width)
    riders = split_parts(direction, local_width)
    block = jnp.concatenate([attended, riders], axis=0)
    near = ring_gathered(ring_gathered(block[None], "x"), "y")
    far = lax.ppermute(near, "core", [(0, 1), (1, 0)])

    offsets = jnp.arange(RING, dtype=jnp.int32)
    origin_x = (lax.axis_index("x") + offsets) % RING
    origin_y = (lax.axis_index("y") + offsets) % RING
    near_origin = ((origin_x[None, :] * RING + origin_y[:, None]) * 2).reshape(-1)
    core_index = lax.axis_index("core")
    origin = jnp.concatenate([near_origin + core_index, near_origin + (1 - core_index)])
    slots = origin.shape[0]
    weight_slots = jnp.take(
        out_weight.reshape(model_cols, slots, local_width), origin, axis=1, mode="clip"
    )
    half = near.shape[0]
    projected = lax.dot_general(
        near,
        weight_slots[:, :half],
        (((0, 2), (1, 2)), ((), ())),
        preferred_element_type=jnp.float32,
    ) + lax.dot_general(
        far,
        weight_slots[:, half:],
        (((0, 2), (1, 2)), ((), ())),
        preferred_element_type=jnp.float32,
    )
    projected = projected.astype(jnp.bfloat16)[:block_rows]
    rider_rows = jnp.concatenate(
        [near[:, block_rows : block_rows + PARTS], far[:, block_rows : block_rows + PARTS]], axis=0
    )
    reorder = (origin[None, :] == jnp.arange(slots, dtype=jnp.int32)[:, None]).astype(jnp.bfloat16)
    ordered = jnp.einsum("os,spk->pok", reorder, rider_rows, preferred_element_type=jnp.float32)
    direction_full = joined_parts(ordered.astype(jnp.bfloat16), local_width, model_cols)

    experts_all = lax.axis_size(EP) * EXP_DEV
    capacity = 2 * block_rows * TOP // experts_all
    flat_ids = expert_ids.reshape(-1)
    matches = (flat_ids[:, None] == jnp.arange(experts_all, dtype=jnp.int32)[None, :]).astype(
        jnp.int32
    )
    slot_index = jnp.sum((jnp.cumsum(matches, axis=0) - matches) * matches, axis=1)
    position = (flat_ids * capacity + slot_index).reshape(block_rows, TOP)
    places = jnp.arange(experts_all * capacity, dtype=jnp.int32)[:, None]
    chosen = (position[None, :, 0] == places) | (position[None, :, 1] == places)
    for pick in range(2, TOP):
        chosen = chosen | (position[None, :, pick] == places)
    tile_rows = jnp.dot(
        chosen.astype(jnp.bfloat16), projected, preferred_element_type=jnp.float32
    ).astype(jnp.bfloat16)
    tile_rows = tile_rows.reshape(experts_all, capacity, model_cols)
    received = lax.all_to_all(tile_rows, EP, split_axis=0, concat_axis=2, tiled=True)

    local_flags = flagged - ctx_index * block_rows
    token_flag = jnp.any(
        local_flags[None, :] == jnp.arange(block_rows, dtype=jnp.int32)[:, None], axis=1
    )
    owned = ((expert_ids // EXP_DEV == ep_index) & token_flag[:, None]).reshape(-1)
    slot_ids = (flat_ids % EXP_DEV) * capacity + slot_index
    slot_flag = jnp.any(
        owned[None, :]
        & (slot_ids[None, :] == jnp.arange(EXP_DEV * capacity, dtype=jnp.int32)[:, None]),
        axis=1,
    ).reshape(EXP_DEV, capacity)

    norm_square = jnp.sum(direction_full * direction_full) + 1e-06
    rows = received.astype(jnp.float32)
    products = jnp.einsum("ecm,m->ec", rows, direction_full, precision=lax.Precision.HIGHEST)
    removed = (
        rows - (products / norm_square)[:, :, None] * direction_full[None, None, :]
    ).astype(jnp.bfloat16)
    return jnp.where(slot_flag[:, :, None], removed, received)


def solution(mesh):
    devices = np.asarray(mesh.devices)
    fine = Mesh(devices.reshape(devices.shape[0], RING, RING, 2), ("ctx",) + EP)
    placed = (
        P("ctx", EP),
        P("ctx", EP),
        P("ctx", EP),
        P("ctx", EP),
        P(EP, None),
        P("ctx", None),
        P("ctx"),
        P(EP),
    )
    return jax.shard_map(
        local, mesh=fine, in_specs=placed, out_specs=P(EP, "ctx", None), check_vma=False
    )
```

```python
import jax
import jax.numpy as jnp
import numpy as np
from jax import lax
from jax.sharding import Mesh
from jax.sharding import PartitionSpec as P

HEAD = 128
TOP = 2
EXP_DEV = 1
SUB = 256
PAD_ROWS = 8
PARTS = 3
RING = 4
EP = ("x", "y", "core")


def local_step(carried_in, pieces):
    kv_state, offset = carried_in
    query_sub, key_sub, value_sub, decay_sub = pieces
    sub_rows = query_sub.shape[0]
    cumulated = jnp.cumsum(decay_sub, axis=0)
    scores = jnp.einsum("thd,shd->hts", query_sub, key_sub, preferred_element_type=jnp.float32)
    spread = jnp.transpose(cumulated)
    decay_gaps = jnp.minimum(spread[:, :, None] - spread[:, None, :], 0.0)
    causal = (
        jnp.arange(sub_rows, dtype=jnp.int32)[:, None]
        >= jnp.arange(sub_rows, dtype=jnp.int32)[None, :]
    )
    weights = jnp.where(causal[None], scores * jnp.exp(decay_gaps), 0.0).astype(jnp.bfloat16)
    inside = jnp.einsum("hts,shd->thd", weights, value_sub, preferred_element_type=jnp.float32)
    scaled = query_sub.astype(jnp.float32) * jnp.exp(cumulated)[:, :, None]
    carried = jnp.einsum("thd,hde->the", scaled, kv_state, precision=lax.Precision.HIGHEST)
    last_decay = cumulated[-1]
    key_scaled = (
        key_sub.astype(jnp.float32) * jnp.exp(last_decay[None, :] - cumulated)[:, :, None]
    ).astype(jnp.bfloat16)
    update = jnp.einsum("shd,she->hde", key_scaled, value_sub, preferred_element_type=jnp.float32)
    kv_state = jnp.exp(last_decay)[:, None, None] * kv_state + update
    reach_decay = jnp.exp(offset[None, :] + cumulated)
    return ((kv_state, offset + last_decay), (inside + carried, reach_decay))


def normalize(outputs):
    mean_square = jnp.mean(outputs * outputs, axis=-1, keepdims=True)
    return (outputs * lax.rsqrt(mean_square + 1e-06)).astype(jnp.bfloat16)


def combined(left, right):
    right_log = right[:, HEAD:, :]
    gain = jnp.exp(right_log[:, :1, :1])
    state = gain * left[:, :HEAD, :] + right[:, :HEAD, :]
    return jnp.concatenate([state, right_log + left[:, HEAD:, :]], axis=1)


def ring_gathered(blocks, axis):
    def shifted(value, steps):
        return lax.ppermute(value, axis, [(i, (i + steps) % RING) for i in range(RING)])

    half = blocks.shape[-1] // 2
    from_right = shifted(blocks, -1)
    from_left = shifted(blocks, 1)
    far = jnp.concatenate([shifted(blocks[..., :half], 2), shifted(blocks[..., half:], -2)], axis=-1)
    return jnp.concatenate([blocks, from_right, far, from_left], axis=0)


def received_by(pairs, count, position):
    table = [False] * count
    for _, target in pairs:
        table[target] = True
    return jnp.asarray(table)[position]


def exclusive_scan(value, axis, count):
    position = lax.axis_index(axis)
    if count == 1:
        return jnp.zeros_like(value)

    def step(current, pairs, merge):
        arrived = lax.ppermute(current, axis, pairs)
        return arrived, jnp.where(received_by(pairs, count, position), merge(arrived), current)

    segment = value
    left_raw = None
    distance = 1
    while 4 * distance <= count:
        pairs = [(j - distance, j) for j in range(count) if (j + 1) % (2 * distance) == 0]
        arrived, segment = step(segment, pairs, lambda got, seg=segment: combined(got, seg))
        if left_raw is None:
            left_raw = arrived
        distance *= 2
    distance //= 2
    while distance >= 2:
        pairs = [
            (j, j + distance)
            for j in range(count)
            if (j + 1) % (2 * distance) == 0 and j + distance < count
        ]
        _, segment = step(segment, pairs, lambda got, seg=segment: combined(got, seg))
        distance //= 2
    if left_raw is None:
        left_raw = lax.ppermute(segment, axis, [(j - 1, j) for j in range(1, count, 2)])
    to_even = [(j, j + 1) for j in range(1, count - 1, 2)]
    to_odd = [(j, j + 2) for j in range(1, count - 2, 2)]
    from_odd = lax.ppermute(segment, axis, to_even)
    from_odd_far = lax.ppermute(segment, axis, to_odd)
    odd_result = jnp.where(position >= 3, combined(from_odd_far, left_raw), left_raw)
    result = jnp.where(position % 2 == 1, odd_result, from_odd)
    return jnp.where(position == 0, jnp.zeros_like(value), result)


def split_parts(values, width):
    pieces = []
    rest = values
    for _ in range(PARTS):
        part = lax.reduce_precision(rest, exponent_bits=8, mantissa_bits=7)
        pieces.append(part)
        rest = rest - part
    stacked = jnp.stack(pieces).astype(jnp.bfloat16)
    return jnp.pad(stacked, ((0, PAD_ROWS - PARTS), (0, width - values.shape[0])))


def joined_parts(rows, width, used):
    pieces = rows.astype(jnp.float32).reshape(PARTS, -1, width)[:, :, :used].reshape(PARTS, -1)
    total = pieces[0]
    for part in range(1, PARTS):
        total = total + pieces[part]
    return total


def local_body(queries, key_rows, value_rows, log_decay, out_weight, expert_ids, flagged, direction):
    block_rows = queries.shape[0]
    local_width = queries.shape[1]
    local_heads = local_width // HEAD
    sub_count = block_rows // SUB
    model_cols = out_weight.shape[0]
    ctx_count = lax.axis_size("ctx")
    ctx_index = lax.axis_index("ctx")
    ep_index = lax.axis_index(EP)

    def shaped(operand):
        return operand.reshape(sub_count, SUB, local_heads, HEAD)

    start_state = (
        jnp.zeros((local_heads, HEAD, HEAD), jnp.float32),
        jnp.zeros((local_heads,), jnp.float32),
    )
    scanned = lax.scan(
        local_step,
        start_state,
        (
            shaped(queries),
            shaped(key_rows),
            shaped(value_rows),
            log_decay.reshape(sub_count, SUB, local_heads),
        ),
    )
    local_state, total_decay = scanned[0]
    partial_out, reach_decay = scanned[1]

    packed = jnp.concatenate(
        [local_state, jnp.broadcast_to(total_decay[:, None, None], (local_heads, PAD_ROWS, HEAD))],
        axis=1,
    )
    exclusive = exclusive_scan(packed, "ctx", ctx_count)
    incoming = exclusive[:, :HEAD, :]

    scaled = shaped(queries).astype(jnp.float32) * reach_decay[..., None]
    outputs = partial_out + jnp.einsum(
        "cthd,hde->cthe", scaled, incoming, precision=lax.Precision.HIGHEST
    )
    attended = normalize(outputs).reshape(block_rows, local_width)
    riders = split_parts(direction, local_width)
    block = jnp.concatenate([attended, riders], axis=0)
    near = ring_gathered(ring_gathered(block[None], "x"), "y")
    far = lax.ppermute(near, "core", [(0, 1), (1, 0)])

    offsets = jnp.arange(RING, dtype=jnp.int32)
    origin_x = (lax.axis_index("x") + offsets) % RING
    origin_y = (lax.axis_index("y") + offsets) % RING
    near_origin = ((origin_x[None, :] * RING + origin_y[:, None]) * 2).reshape(-1)
    core_index = lax.axis_index("core")
    origin = jnp.concatenate([near_origin + core_index, near_origin + (1 - core_index)])
    slots = origin.shape[0]
    weight_slots = jnp.take(
        out_weight.reshape(model_cols, slots, local_width), origin, axis=1, mode="clip"
    )
    half = near.shape[0]
    projected = lax.dot_general(
        near,
        weight_slots[:, :half],
        (((0, 2), (1, 2)), ((), ())),
        preferred_element_type=jnp.float32,
    ) + lax.dot_general(
        far,
        weight_slots[:, half:],
        (((0, 2), (1, 2)), ((), ())),
        preferred_element_type=jnp.float32,
    )
    projected = projected.astype(jnp.bfloat16)[:block_rows]
    rider_rows = jnp.concatenate(
        [near[:, block_rows : block_rows + PARTS], far[:, block_rows : block_rows + PARTS]], axis=0
    )
    reorder = (origin[None, :] == jnp.arange(slots, dtype=jnp.int32)[:, None]).astype(jnp.bfloat16)
    ordered = jnp.einsum("os,spk->pok", reorder, rider_rows, preferred_element_type=jnp.float32)
    direction_full = joined_parts(ordered.astype(jnp.bfloat16), local_width, model_cols)

    experts_all = lax.axis_size(EP) * EXP_DEV
    capacity = 2 * block_rows * TOP // experts_all
    flat_ids = expert_ids.reshape(-1)
    matches = (flat_ids[:, None] == jnp.arange(experts_all, dtype=jnp.int32)[None, :]).astype(
        jnp.int32
    )
    slot_index = jnp.sum((jnp.cumsum(matches, axis=0) - matches) * matches, axis=1)
    position = (flat_ids * capacity + slot_index).reshape(block_rows, TOP)
    places = jnp.arange(experts_all * capacity, dtype=jnp.int32)[:, None]
    chosen = (position[None, :, 0] == places) | (position[None, :, 1] == places)
    for pick in range(2, TOP):
        chosen = chosen | (position[None, :, pick] == places)
    tile_rows = jnp.dot(
        chosen.astype(jnp.bfloat16), projected, preferred_element_type=jnp.float32
    ).astype(jnp.bfloat16)
    tile_rows = tile_rows.reshape(experts_all, capacity, model_cols)
    received = lax.all_to_all(tile_rows, EP, split_axis=0, concat_axis=2, tiled=True)

    local_flags = flagged - ctx_index * block_rows
    token_flag = jnp.any(
        local_flags[None, :] == jnp.arange(block_rows, dtype=jnp.int32)[:, None], axis=1
    )
    owned = ((expert_ids // EXP_DEV == ep_index) & token_flag[:, None]).reshape(-1)
    slot_ids = (flat_ids % EXP_DEV) * capacity + slot_index
    slot_flag = jnp.any(
        owned[None, :]
        & (slot_ids[None, :] == jnp.arange(EXP_DEV * capacity, dtype=jnp.int32)[:, None]),
        axis=1,
    ).reshape(EXP_DEV, capacity)

    norm_square = jnp.sum(direction_full * direction_full) + 1e-06
    rows = received.astype(jnp.float32)
    products = jnp.einsum("ecm,m->ec", rows, direction_full, precision=lax.Precision.HIGHEST)
    removed = (
        rows - (products / norm_square)[:, :, None] * direction_full[None, None, :]
    ).astype(jnp.bfloat16)
    return jnp.where(slot_flag[:, :, None], removed, received)


def solution(mesh):
    devices = np.asarray(mesh.devices)
    fine = Mesh(devices.reshape(devices.shape[0], RING, RING, 2), ("ctx",) + EP)
    placed = (
        P("ctx", EP),
        P("ctx", EP),
        P("ctx", EP),
        P("ctx", EP),
        P(EP, None),
        P("ctx", None),
        P("ctx"),
        P(EP),
    )
    return jax.shard_map(
        local_body, mesh=fine, in_specs=placed, out_specs=P(EP, "ctx", None), check_vma=False
    )
```

```python
import jax
import jax.numpy as jnp
import numpy as np
from jax import lax
from jax.sharding import Mesh
from jax.sharding import PartitionSpec as P

HEAD = 128
TOP = 2
EXP_DEV = 1
SUB = 256
PAD_ROWS = 8
PARTS = 3
RING = 4
EP = ("x", "y", "core")


def local_step(carried_in, pieces):
    kv_state, offset = carried_in
    query_sub, key_sub, value_sub, decay_sub = pieces
    sub_rows = query_sub.shape[0]
    cumulated = jnp.cumsum(decay_sub, axis=0)
    scores = jnp.einsum("thd,shd->hts", query_sub, key_sub, preferred_element_type=jnp.float32)
    spread = jnp.transpose(cumulated)
    decay_gaps = jnp.minimum(spread[:, :, None] - spread[:, None, :], 0.0)
    causal = (
        jnp.arange(sub_rows, dtype=jnp.int32)[:, None]
        >= jnp.arange(sub_rows, dtype=jnp.int32)[None, :]
    )
    weights = jnp.where(causal[None], scores * jnp.exp(decay_gaps), 0.0).astype(jnp.bfloat16)
    inside = jnp.einsum("hts,shd->thd", weights, value_sub, preferred_element_type=jnp.float32)
    scaled = query_sub.astype(jnp.float32) * jnp.exp(cumulated)[:, :, None]
    carried = jnp.einsum("thd,hde->the", scaled, kv_state, precision=lax.Precision.HIGHEST)
    last_decay = cumulated[-1]
    key_scaled = (
        key_sub.astype(jnp.float32) * jnp.exp(last_decay[None, :] - cumulated)[:, :, None]
    ).astype(jnp.bfloat16)
    update = jnp.einsum("shd,she->hde", key_scaled, value_sub, preferred_element_type=jnp.float32)
    kv_state = jnp.exp(last_decay)[:, None, None] * kv_state + update
    reach_decay = jnp.exp(offset[None, :] + cumulated)
    return ((kv_state, offset + last_decay), (inside + carried, reach_decay))


def normalize(outputs):
    mean_square = jnp.mean(outputs * outputs, axis=-1, keepdims=True)
    return (outputs * lax.rsqrt(mean_square + 1e-06)).astype(jnp.bfloat16)


def combined(left, right):
    right_log = right[:, HEAD:, :]
    gain = jnp.exp(right_log[:, :1, :1])
    state = gain * left[:, :HEAD, :] + right[:, :HEAD, :]
    return jnp.concatenate([state, right_log + left[:, HEAD:, :]], axis=1)


def ring_gathered(blocks, axis):
    def shifted(value, steps):
        return lax.ppermute(value, axis, [(i, (i + steps) % RING) for i in range(RING)])

    half = blocks.shape[-1] // 2
    from_right = shifted(blocks, -1)
    from_left = shifted(blocks, 1)
    far = jnp.concatenate([shifted(blocks[..., :half], 2), shifted(blocks[..., half:], -2)], axis=-1)
    return jnp.concatenate([blocks, from_right, far, from_left], axis=0)


def exclusive_scan(value, axis, count):
    position = lax.axis_index(axis)
    if count == 1:
        return jnp.zeros_like(value)

    def step(current, pairs, chosen, merge):
        arrived = lax.ppermute(current, axis, pairs)
        return arrived, jnp.where(chosen, merge(arrived), current)

    segment = value
    left_raw = None
    distance = 1
    while 4 * distance <= count:
        pairs = [(j - distance, j) for j in range(count) if (j + 1) % (2 * distance) == 0]
        chosen = (position + 1) % (2 * distance) == 0
        arrived, segment = step(segment, pairs, chosen, lambda got, seg=segment: combined(got, seg))
        if left_raw is None:
            left_raw = arrived
        distance *= 2
    distance //= 2
    while distance >= 2:
        pairs = [
            (j, j + distance)
            for j in range(count)
            if (j + 1) % (2 * distance) == 0 and j + distance < count
        ]
        chosen = ((position + 1 - distance) % (2 * distance) == 0) & (position >= 3 * distance - 1)
        _, segment = step(segment, pairs, chosen, lambda got, seg=segment: combined(got, seg))
        distance //= 2
    if left_raw is None:
        left_raw = lax.ppermute(segment, axis, [(j - 1, j) for j in range(1, count, 2)])
    to_even = [(j, j + 1) for j in range(1, count - 1, 2)]
    to_odd = [(j, j + 2) for j in range(1, count - 2, 2)]
    from_odd = lax.ppermute(segment, axis, to_even)
    from_odd_far = lax.ppermute(segment, axis, to_odd)
    odd_result = jnp.where(position >= 3, combined(from_odd_far, left_raw), left_raw)
    result = jnp.where(position % 2 == 1, odd_result, from_odd)
    return jnp.where(position == 0, jnp.zeros_like(value), result)


def split_parts(values, width):
    pieces = []
    rest = values
    for _ in range(PARTS):
        part = lax.reduce_precision(rest, exponent_bits=8, mantissa_bits=7)
        pieces.append(part)
        rest = rest - part
    stacked = jnp.stack(pieces).astype(jnp.bfloat16)
    return jnp.pad(stacked, ((0, PAD_ROWS - PARTS), (0, width - values.shape[0])))


def joined_parts(rows, width, used):
    pieces = rows.astype(jnp.float32).reshape(PARTS, -1, width)[:, :, :used].reshape(PARTS, -1)
    total = pieces[0]
    for part in range(1, PARTS):
        total = total + pieces[part]
    return total


def local_body(queries, key_rows, value_rows, log_decay, out_weight, expert_ids, flagged, direction):
    block_rows = queries.shape[0]
    local_width = queries.shape[1]
    local_heads = local_width // HEAD
    sub_count = block_rows // SUB
    model_cols = out_weight.shape[0]
    ctx_count = lax.axis_size("ctx")
    ctx_index = lax.axis_index("ctx")
    ep_index = lax.axis_index(EP)

    def shaped(operand):
        return operand.reshape(sub_count, SUB, local_heads, HEAD)

    start_state = (
        jnp.zeros((local_heads, HEAD, HEAD), jnp.float32),
        jnp.zeros((local_heads,), jnp.float32),
    )
    scanned = lax.scan(
        local_step,
        start_state,
        (
            shaped(queries),
            shaped(key_rows),
            shaped(value_rows),
            log_decay.reshape(sub_count, SUB, local_heads),
        ),
    )
    local_state, total_decay = scanned[0]
    partial_out, reach_decay = scanned[1]

    packed = jnp.concatenate(
        [local_state, jnp.broadcast_to(total_decay[:, None, None], (local_heads, PAD_ROWS, HEAD))],
        axis=1,
    )
    exclusive = exclusive_scan(packed, "ctx", ctx_count)
    incoming = exclusive[:, :HEAD, :]

    scaled = shaped(queries).astype(jnp.float32) * reach_decay[..., None]
    outputs = partial_out + jnp.einsum(
        "cthd,hde->cthe", scaled, incoming, precision=lax.Precision.HIGHEST
    )
    attended = normalize(outputs).reshape(block_rows, local_width)
    riders = split_parts(direction, local_width)
    block = jnp.concatenate([attended, riders], axis=0)
    near = ring_gathered(block[None], "x")
    near = ring_gathered(near, "y")
    far = lax.ppermute(near, "core", [(0, 1), (1, 0)])

    offsets = jnp.arange(RING, dtype=jnp.int32)
    origin_x = (lax.axis_index("x") + offsets) % RING
    origin_y = (lax.axis_index("y") + offsets) % RING
    near_origin = ((origin_x[None, :] * RING + origin_y[:, None]) * 2).reshape(-1)
    core_index = lax.axis_index("core")
    origin = jnp.concatenate([near_origin + core_index, near_origin + (1 - core_index)])
    slots = origin.shape[0]
    weight_slots = jnp.take(
        out_weight.reshape(model_cols, slots, local_width), origin, axis=1, mode="clip"
    )
    half = near.shape[0]
    projected = lax.dot_general(
        near[:, :block_rows],
        weight_slots[:, :half],
        (((0, 2), (1, 2)), ((), ())),
        preferred_element_type=jnp.float32,
    ) + lax.dot_general(
        far[:, :block_rows],
        weight_slots[:, half:],
        (((0, 2), (1, 2)), ((), ())),
        preferred_element_type=jnp.float32,
    )
    projected = projected.astype(jnp.bfloat16)
    rider_rows = jnp.concatenate(
        [near[:, block_rows : block_rows + PARTS], far[:, block_rows : block_rows + PARTS]], axis=0
    )
    reorder = (origin[None, :] == jnp.arange(slots, dtype=jnp.int32)[:, None]).astype(jnp.bfloat16)
    ordered = jnp.einsum("os,spk->pok", reorder, rider_rows, preferred_element_type=jnp.float32)
    direction_full = joined_parts(ordered.astype(jnp.bfloat16), local_width, model_cols)

    experts_all = lax.axis_size(EP) * EXP_DEV
    capacity = 2 * block_rows * TOP // experts_all
    flat_ids = expert_ids.reshape(-1)
    matches = (flat_ids[:, None] == jnp.arange(experts_all, dtype=jnp.int32)[None, :]).astype(
        jnp.int32
    )
    slot_index = jnp.sum((jnp.cumsum(matches, axis=0) - matches) * matches, axis=1)
    position = (flat_ids * capacity + slot_index).reshape(block_rows, TOP)
    places = jnp.arange(experts_all * capacity, dtype=jnp.int32)[:, None]
    chosen = (position[None, :, 0] == places) | (position[None, :, 1] == places)
    for pick in range(2, TOP):
        chosen = chosen | (position[None, :, pick] == places)
    tile_rows = jnp.dot(
        chosen.astype(jnp.bfloat16), projected, preferred_element_type=jnp.float32
    ).astype(jnp.bfloat16)
    tile_rows = tile_rows.reshape(experts_all, capacity, model_cols)
    received = lax.all_to_all(tile_rows, EP, split_axis=0, concat_axis=2, tiled=True)

    local_flags = flagged - ctx_index * block_rows
    token_flag = jnp.any(
        local_flags[None, :] == jnp.arange(block_rows, dtype=jnp.int32)[:, None], axis=1
    )
    owned = ((expert_ids // EXP_DEV == ep_index) & token_flag[:, None]).reshape(-1)
    slot_ids = (flat_ids % EXP_DEV) * capacity + slot_index
    slot_flag = jnp.any(
        owned[None, :]
        & (slot_ids[None, :] == jnp.arange(EXP_DEV * capacity, dtype=jnp.int32)[:, None]),
        axis=1,
    ).reshape(EXP_DEV, capacity)

    norm_square = jnp.sum(direction_full * direction_full) + 1e-06
    rows = received.astype(jnp.float32)
    products = jnp.einsum("ecm,m->ec", rows, direction_full, precision=lax.Precision.HIGHEST)
    removed = (
        rows - (products / norm_square)[:, :, None] * direction_full[None, None, :]
    ).astype(jnp.bfloat16)
    return jnp.where(slot_flag[:, :, None], removed, received)


def solution(mesh):
    devices = np.asarray(mesh.devices)
    fine = Mesh(devices.reshape(devices.shape[0], RING, RING, 2), ("ctx",) + EP)
    placed = (
        P("ctx", EP),
        P("ctx", EP),
        P("ctx", EP),
        P("ctx", EP),
        P(EP, None),
        P("ctx", None),
        P("ctx"),
        P(EP),
    )
    return jax.shard_map(
        local_body, mesh=fine, in_specs=placed, out_specs=P(EP, "ctx", None), check_vma=False
    )
```

```python
import jax
import jax.numpy as jnp
import numpy as np
from jax import lax
from jax.sharding import Mesh
from jax.sharding import PartitionSpec as P

HEAD = 128
TOP = 2
EXP_DEV = 1
SUB = 256
PAD_ROWS = 8
PARTS = 3
RING = 4
EP = ("x", "y", "core")


def local_step(carried_in, pieces):
    kv_state, offset = carried_in
    query_sub, key_sub, value_sub, decay_sub = pieces
    sub_rows = query_sub.shape[0]
    cumulated = jnp.cumsum(decay_sub, axis=0)
    scores = jnp.einsum("thd,shd->hts", query_sub, key_sub, preferred_element_type=jnp.float32)
    spread = jnp.transpose(cumulated)
    decay_gaps = jnp.minimum(spread[:, :, None] - spread[:, None, :], 0.0)
    causal = (
        jnp.arange(sub_rows, dtype=jnp.int32)[:, None]
        >= jnp.arange(sub_rows, dtype=jnp.int32)[None, :]
    )
    weights = jnp.where(causal[None], scores * jnp.exp(decay_gaps), 0.0).astype(jnp.bfloat16)
    inside = jnp.einsum("hts,shd->thd", weights, value_sub, preferred_element_type=jnp.float32)
    scaled = query_sub.astype(jnp.float32) * jnp.exp(cumulated)[:, :, None]
    carried = jnp.einsum("thd,hde->the", scaled, kv_state, precision=lax.Precision.HIGHEST)
    last_decay = cumulated[-1]
    key_scaled = (
        key_sub.astype(jnp.float32) * jnp.exp(last_decay[None, :] - cumulated)[:, :, None]
    ).astype(jnp.bfloat16)
    update = jnp.einsum("shd,she->hde", key_scaled, value_sub, preferred_element_type=jnp.float32)
    kv_state = jnp.exp(last_decay)[:, None, None] * kv_state + update
    reach_decay = jnp.exp(offset[None, :] + cumulated)
    return ((kv_state, offset + last_decay), (inside + carried, reach_decay))


def normalize(outputs):
    mean_square = jnp.mean(outputs * outputs, axis=-1, keepdims=True)
    return (outputs * lax.rsqrt(mean_square + 1e-06)).astype(jnp.bfloat16)


def combined(left, right):
    right_log = right[:, HEAD:, :]
    gain = jnp.exp(right_log[:, :1, :1])
    state = gain * left[:, :HEAD, :] + right[:, :HEAD, :]
    return jnp.concatenate([state, right_log + left[:, HEAD:, :]], axis=1)


def ring_gathered(blocks, axis):
    def shifted(value, steps):
        return lax.ppermute(value, axis, [(i, (i + steps) % RING) for i in range(RING)])

    half = blocks.shape[-1] // 2
    from_right = shifted(blocks, -1)
    from_left = shifted(blocks, 1)
    far = jnp.concatenate([shifted(blocks[..., :half], 2), shifted(blocks[..., half:], -2)], axis=-1)
    return jnp.concatenate([blocks, from_right, far, from_left], axis=0)


def exclusive_scan(value, axis, count):
    position = lax.axis_index(axis)
    if count == 1:
        return jnp.zeros_like(value)

    def step(current, pairs, chosen, merge):
        arrived = lax.ppermute(current, axis, pairs)
        return arrived, jnp.where(chosen, merge(arrived), current)

    segment = value
    left_raw = None
    distance = 1
    while 4 * distance <= count:
        pairs = [(j - distance, j) for j in range(count) if (j + 1) % (2 * distance) == 0]
        chosen = (position + 1) % (2 * distance) == 0
        arrived, segment = step(segment, pairs, chosen, lambda got, seg=segment: combined(got, seg))
        if left_raw is None:
            left_raw = arrived
        distance *= 2
    distance //= 2
    while distance >= 2:
        pairs = [
            (j, j + distance)
            for j in range(count)
            if (j + 1) % (2 * distance) == 0 and j + distance < count
        ]
        chosen = ((position + 1 - distance) % (2 * distance) == 0) & (position >= 3 * distance - 1)
        _, segment = step(segment, pairs, chosen, lambda got, seg=segment: combined(got, seg))
        distance //= 2
    if left_raw is None:
        left_raw = lax.ppermute(segment, axis, [(j - 1, j) for j in range(1, count, 2)])
    to_even = [(j, j + 1) for j in range(1, count - 1, 2)]
    to_odd = [(j, j + 2) for j in range(1, count - 2, 2)]
    from_odd = lax.ppermute(segment, axis, to_even)
    from_odd_far = lax.ppermute(segment, axis, to_odd)
    odd_result = jnp.where(position >= 3, combined(from_odd_far, left_raw), left_raw)
    result = jnp.where(position % 2 == 1, odd_result, from_odd)
    return jnp.where(position == 0, jnp.zeros_like(value), result)


def split_parts(values, width):
    pieces = []
    rest = values
    for _ in range(PARTS):
        part = lax.reduce_precision(rest, exponent_bits=8, mantissa_bits=7)
        pieces.append(part)
        rest = rest - part
    stacked = jnp.stack(pieces).astype(jnp.bfloat16)
    return jnp.pad(stacked, ((0, PAD_ROWS - PARTS), (0, width - values.shape[0])))


def joined_parts(rows, width, used):
    pieces = rows.astype(jnp.float32).reshape(PARTS, -1, width)[:, :, :used].reshape(PARTS, -1)
    total = pieces[0]
    for part in range(1, PARTS):
        total = total + pieces[part]
    return total


def local_body(queries, key_rows, value_rows, log_decay, out_weight, expert_ids, flagged, direction):
    block_rows = queries.shape[0]
    local_width = queries.shape[1]
    local_heads = local_width // HEAD
    sub_count = block_rows // SUB
    model_cols = out_weight.shape[0]
    ctx_count = lax.axis_size("ctx")
    ctx_index = lax.axis_index("ctx")
    ep_index = lax.axis_index(EP)

    def shaped(operand):
        return operand.reshape(sub_count, SUB, local_heads, HEAD)

    start_state = (
        jnp.zeros((local_heads, HEAD, HEAD), jnp.float32),
        jnp.zeros((local_heads,), jnp.float32),
    )
    scanned = lax.scan(
        local_step,
        start_state,
        (
            shaped(queries),
            shaped(key_rows),
            shaped(value_rows),
            log_decay.reshape(sub_count, SUB, local_heads),
        ),
    )
    local_state, total_decay = scanned[0]
    partial_out, reach_decay = scanned[1]

    packed = jnp.concatenate(
        [local_state, jnp.broadcast_to(total_decay[:, None, None], (local_heads, PAD_ROWS, HEAD))],
        axis=1,
    )
    exclusive = exclusive_scan(packed, "ctx", ctx_count)
    incoming = exclusive[:, :HEAD, :]

    scaled = shaped(queries).astype(jnp.float32) * reach_decay[..., None]
    outputs = partial_out + jnp.einsum(
        "cthd,hde->cthe", scaled, incoming, precision=lax.Precision.HIGHEST
    )
    attended = normalize(outputs).reshape(block_rows, local_width)
    riders = split_parts(direction, local_width)
    block = jnp.concatenate([attended, riders], axis=0)
    near = ring_gathered(block[None], "x")
    near = ring_gathered(near, "y")

    core_index = lax.axis_index("core")
    chips = RING * RING
    own_weight = out_weight.reshape(model_cols, chips, 2, local_width)
    partner_all = lax.ppermute(out_weight, "core", [(0, 1), (1, 0)])
    partner_weight = lax.dynamic_index_in_dim(
        partner_all.reshape(own_weight.shape), core_index, axis=2, keepdims=False
    )

    offsets = jnp.arange(RING, dtype=jnp.int32)
    origin_x = (lax.axis_index("x") + offsets) % RING
    origin_y = (lax.axis_index("y") + offsets) % RING
    chip_origin = (origin_x[None, :] * RING + origin_y[:, None]).reshape(-1)
    mine = lax.dynamic_index_in_dim(own_weight, core_index, axis=2, keepdims=False)
    both = jnp.concatenate([mine, partner_weight], axis=0)
    weight_slots = jnp.take(both, chip_origin, axis=1, mode="clip")
    partial = lax.dot_general(
        near,
        weight_slots,
        (((0, 2), (1, 2)), ((), ())),
        preferred_element_type=jnp.float32,
    )
    own_riders = near[:, block_rows : block_rows + PARTS]
    outgoing = jnp.concatenate(
        [
            partial[:block_rows, model_cols:],
            own_riders.astype(jnp.float32).reshape(-1, model_cols),
        ],
        axis=0,
    )
    incoming_partial = lax.ppermute(outgoing, "core", [(0, 1), (1, 0)])
    projected = (partial[:block_rows, :model_cols] + incoming_partial[:block_rows]).astype(
        jnp.bfloat16
    )
    partner_riders = incoming_partial[block_rows:].reshape(own_riders.shape).astype(jnp.bfloat16)
    near_origin = chip_origin * 2
    origin = jnp.concatenate([near_origin + core_index, near_origin + (1 - core_index)])
    slots = origin.shape[0]
    rider_rows = jnp.concatenate([own_riders, partner_riders], axis=0)
    reorder = (origin[None, :] == jnp.arange(slots, dtype=jnp.int32)[:, None]).astype(jnp.bfloat16)
    ordered = jnp.einsum("os,spk->pok", reorder, rider_rows, preferred_element_type=jnp.float32)
    direction_full = joined_parts(ordered.astype(jnp.bfloat16), local_width, model_cols)

    experts_all = lax.axis_size(EP) * EXP_DEV
    capacity = 2 * block_rows * TOP // experts_all
    flat_ids = expert_ids.reshape(-1)
    matches = (flat_ids[:, None] == jnp.arange(experts_all, dtype=jnp.int32)[None, :]).astype(
        jnp.int32
    )
    slot_index = jnp.sum((jnp.cumsum(matches, axis=0) - matches) * matches, axis=1)
    position = (flat_ids * capacity + slot_index).reshape(block_rows, TOP)
    places = jnp.arange(experts_all * capacity, dtype=jnp.int32)[:, None]
    chosen = (position[None, :, 0] == places) | (position[None, :, 1] == places)
    for pick in range(2, TOP):
        chosen = chosen | (position[None, :, pick] == places)
    tile_rows = jnp.dot(
        chosen.astype(jnp.bfloat16), projected, preferred_element_type=jnp.float32
    ).astype(jnp.bfloat16)
    tile_rows = tile_rows.reshape(experts_all, capacity, model_cols)
    received = lax.all_to_all(tile_rows, EP, split_axis=0, concat_axis=2, tiled=True)

    local_flags = flagged - ctx_index * block_rows
    token_flag = jnp.any(
        local_flags[None, :] == jnp.arange(block_rows, dtype=jnp.int32)[:, None], axis=1
    )
    owned = ((expert_ids // EXP_DEV == ep_index) & token_flag[:, None]).reshape(-1)
    slot_ids = (flat_ids % EXP_DEV) * capacity + slot_index
    slot_flag = jnp.any(
        owned[None, :]
        & (slot_ids[None, :] == jnp.arange(EXP_DEV * capacity, dtype=jnp.int32)[:, None]),
        axis=1,
    ).reshape(EXP_DEV, capacity)

    norm_square = jnp.sum(direction_full * direction_full) + 1e-06
    rows = received.astype(jnp.float32)
    products = jnp.einsum("ecm,m->ec", rows, direction_full, precision=lax.Precision.HIGHEST)
    removed = (
        rows - (products / norm_square)[:, :, None] * direction_full[None, None, :]
    ).astype(jnp.bfloat16)
    return jnp.where(slot_flag[:, :, None], removed, received)


def solution(mesh):
    devices = np.asarray(mesh.devices)
    fine = Mesh(devices.reshape(devices.shape[0], RING, RING, 2), ("ctx",) + EP)
    placed = (
        P("ctx", EP),
        P("ctx", EP),
        P("ctx", EP),
        P("ctx", EP),
        P(EP, None),
        P("ctx", None),
        P("ctx"),
        P(EP),
    )
    return jax.shard_map(
        local_body, mesh=fine, in_specs=placed, out_specs=P(EP, "ctx", None), check_vma=False
    )
```

```python
import jax
import jax.numpy as jnp
import numpy as np
from jax import lax
from jax.sharding import Mesh
from jax.sharding import PartitionSpec as P

HEAD = 128
TOP = 2
EXP_DEV = 1
SUB = 256
PAD_ROWS = 8
PARTS = 3
RING = 4
EP = ("x", "y", "core")


def local_step(carried_in, pieces):
    kv_state, offset = carried_in
    query_sub, key_sub, value_sub, decay_sub = pieces
    sub_rows = query_sub.shape[0]
    cumulated = jnp.cumsum(decay_sub, axis=0)
    scores = jnp.einsum("thd,shd->hts", query_sub, key_sub, preferred_element_type=jnp.float32)
    spread = jnp.transpose(cumulated)
    decay_gaps = jnp.minimum(spread[:, :, None] - spread[:, None, :], 0.0)
    causal = (
        jnp.arange(sub_rows, dtype=jnp.int32)[:, None]
        >= jnp.arange(sub_rows, dtype=jnp.int32)[None, :]
    )
    weights = jnp.where(causal[None], scores * jnp.exp(decay_gaps), 0.0).astype(jnp.bfloat16)
    inside = jnp.einsum("hts,shd->thd", weights, value_sub, preferred_element_type=jnp.float32)
    scaled = query_sub.astype(jnp.float32) * jnp.exp(cumulated)[:, :, None]
    carried = jnp.einsum("thd,hde->the", scaled, kv_state, precision=lax.Precision.HIGHEST)
    last_decay = cumulated[-1]
    key_scaled = (
        key_sub.astype(jnp.float32) * jnp.exp(last_decay[None, :] - cumulated)[:, :, None]
    ).astype(jnp.bfloat16)
    update = jnp.einsum("shd,she->hde", key_scaled, value_sub, preferred_element_type=jnp.float32)
    kv_state = jnp.exp(last_decay)[:, None, None] * kv_state + update
    reach_decay = jnp.exp(offset[None, :] + cumulated)
    return ((kv_state, offset + last_decay), (inside + carried, reach_decay))


def normalize(outputs):
    mean_square = jnp.mean(outputs * outputs, axis=-1, keepdims=True)
    return (outputs * lax.rsqrt(mean_square + 1e-06)).astype(jnp.bfloat16)


def combined(left, right):
    right_log = right[:, HEAD:, :]
    gain = jnp.exp(right_log[:, :1, :1])
    state = gain * left[:, :HEAD, :] + right[:, :HEAD, :]
    return jnp.concatenate([state, right_log + left[:, HEAD:, :]], axis=1)


def ring_gathered(blocks, axis):
    def shifted(value, steps):
        return lax.ppermute(value, axis, [(i, (i + steps) % RING) for i in range(RING)])

    from_right = shifted(blocks, -1)
    from_left = shifted(blocks, 1)
    if blocks.shape[0] % 2 == 0:
        half = blocks.shape[0] // 2
        far = jnp.concatenate([shifted(blocks[:half], 2), shifted(blocks[half:], -2)], axis=0)
    else:
        half = blocks.shape[-1] // 2
        far = jnp.concatenate(
            [shifted(blocks[..., :half], 2), shifted(blocks[..., half:], -2)], axis=-1
        )
    return jnp.concatenate([blocks, from_right, far, from_left], axis=0)


def exclusive_scan(value, axis, count):
    position = lax.axis_index(axis)
    if count == 1:
        return jnp.zeros_like(value)

    def step(current, pairs, chosen, merge):
        arrived = lax.ppermute(current, axis, pairs)
        return arrived, jnp.where(chosen, merge(arrived), current)

    segment = value
    left_raw = None
    distance = 1
    while 4 * distance <= count:
        pairs = [(j - distance, j) for j in range(count) if (j + 1) % (2 * distance) == 0]
        chosen = (position + 1) % (2 * distance) == 0
        arrived, segment = step(segment, pairs, chosen, lambda got, seg=segment: combined(got, seg))
        if left_raw is None:
            left_raw = arrived
        distance *= 2
    distance //= 2
    while distance >= 2:
        pairs = [
            (j, j + distance)
            for j in range(count)
            if (j + 1) % (2 * distance) == 0 and j + distance < count
        ]
        chosen = ((position + 1 - distance) % (2 * distance) == 0) & (position >= 3 * distance - 1)
        _, segment = step(segment, pairs, chosen, lambda got, seg=segment: combined(got, seg))
        distance //= 2
    if left_raw is None:
        left_raw = lax.ppermute(segment, axis, [(j - 1, j) for j in range(1, count, 2)])
    to_even = [(j, j + 1) for j in range(1, count - 1, 2)]
    to_odd = [(j, j + 2) for j in range(1, count - 2, 2)]
    from_odd = lax.ppermute(segment, axis, to_even)
    from_odd_far = lax.ppermute(segment, axis, to_odd)
    odd_result = jnp.where(position >= 3, combined(from_odd_far, left_raw), left_raw)
    result = jnp.where(position % 2 == 1, odd_result, from_odd)
    return jnp.where(position == 0, jnp.zeros_like(value), result)


def split_parts(values, width):
    pieces = []
    rest = values
    for _ in range(PARTS):
        part = lax.reduce_precision(rest, exponent_bits=8, mantissa_bits=7)
        pieces.append(part)
        rest = rest - part
    stacked = jnp.stack(pieces).astype(jnp.bfloat16)
    return jnp.pad(stacked, ((0, PAD_ROWS - PARTS), (0, width - values.shape[0])))


def joined_parts(rows, width, used):
    pieces = rows.astype(jnp.float32).reshape(PARTS, -1, width)[:, :, :used].reshape(PARTS, -1)
    total = pieces[0]
    for part in range(1, PARTS):
        total = total + pieces[part]
    return total


def local_body(queries, key_rows, value_rows, log_decay, out_weight, expert_ids, flagged, direction):
    block_rows = queries.shape[0]
    local_width = queries.shape[1]
    local_heads = local_width // HEAD
    sub_count = block_rows // SUB
    model_cols = out_weight.shape[0]
    ctx_count = lax.axis_size("ctx")
    ctx_index = lax.axis_index("ctx")
    ep_index = lax.axis_index(EP)

    def shaped(operand):
        return operand.reshape(sub_count, SUB, local_heads, HEAD)

    start_state = (
        jnp.zeros((local_heads, HEAD, HEAD), jnp.float32),
        jnp.zeros((local_heads,), jnp.float32),
    )
    scanned = lax.scan(
        local_step,
        start_state,
        (
            shaped(queries),
            shaped(key_rows),
            shaped(value_rows),
            log_decay.reshape(sub_count, SUB, local_heads),
        ),
    )
    local_state, total_decay = scanned[0]
    partial_out, reach_decay = scanned[1]

    packed = jnp.concatenate(
        [local_state, jnp.broadcast_to(total_decay[:, None, None], (local_heads, PAD_ROWS, HEAD))],
        axis=1,
    )
    exclusive = exclusive_scan(packed, "ctx", ctx_count)
    incoming = exclusive[:, :HEAD, :]

    scaled = shaped(queries).astype(jnp.float32) * reach_decay[..., None]
    outputs = partial_out + jnp.einsum(
        "cthd,hde->cthe", scaled, incoming, precision=lax.Precision.HIGHEST
    )
    attended = normalize(outputs).reshape(block_rows, local_width)
    riders = split_parts(direction, local_width)
    block = jnp.concatenate([attended, riders], axis=0)
    near = ring_gathered(block[None], "x")
    near = ring_gathered(near, "y")
    far = lax.ppermute(near, "core", [(0, 1), (1, 0)])

    offsets = jnp.arange(RING, dtype=jnp.int32)
    origin_x = (lax.axis_index("x") + offsets) % RING
    origin_y = (lax.axis_index("y") + offsets) % RING
    near_origin = ((origin_x[None, :] * RING + origin_y[:, None]) * 2).reshape(-1)
    core_index = lax.axis_index("core")
    origin = jnp.concatenate([near_origin + core_index, near_origin + (1 - core_index)])
    slots = origin.shape[0]
    weight_slots = jnp.take(
        out_weight.reshape(model_cols, slots, local_width), origin, axis=1, mode="clip"
    )
    half = near.shape[0]
    projected = lax.dot_general(
        near,
        weight_slots[:, :half],
        (((0, 2), (1, 2)), ((), ())),
        preferred_element_type=jnp.float32,
    ) + lax.dot_general(
        far,
        weight_slots[:, half:],
        (((0, 2), (1, 2)), ((), ())),
        preferred_element_type=jnp.float32,
    )
    projected = projected.astype(jnp.bfloat16)[:block_rows]
    rider_rows = jnp.concatenate(
        [near[:, block_rows : block_rows + PARTS], far[:, block_rows : block_rows + PARTS]], axis=0
    )
    reorder = (origin[None, :] == jnp.arange(slots, dtype=jnp.int32)[:, None]).astype(jnp.bfloat16)
    ordered = jnp.einsum("os,spk->pok", reorder, rider_rows, preferred_element_type=jnp.float32)
    direction_full = joined_parts(ordered.astype(jnp.bfloat16), local_width, model_cols)

    experts_all = lax.axis_size(EP) * EXP_DEV
    capacity = 2 * block_rows * TOP // experts_all
    flat_ids = expert_ids.reshape(-1)
    matches = (flat_ids[:, None] == jnp.arange(experts_all, dtype=jnp.int32)[None, :]).astype(
        jnp.int32
    )
    slot_index = jnp.sum((jnp.cumsum(matches, axis=0) - matches) * matches, axis=1)
    position = (flat_ids * capacity + slot_index).reshape(block_rows, TOP)
    places = jnp.arange(experts_all * capacity, dtype=jnp.int32)[:, None]
    chosen = (position[None, :, 0] == places) | (position[None, :, 1] == places)
    for pick in range(2, TOP):
        chosen = chosen | (position[None, :, pick] == places)
    tile_rows = jnp.dot(
        chosen.astype(jnp.bfloat16), projected, preferred_element_type=jnp.float32
    ).astype(jnp.bfloat16)
    tile_rows = tile_rows.reshape(experts_all, capacity, model_cols)
    received = lax.all_to_all(tile_rows, EP, split_axis=0, concat_axis=2, tiled=True)

    local_flags = flagged - ctx_index * block_rows
    token_flag = jnp.any(
        local_flags[None, :] == jnp.arange(block_rows, dtype=jnp.int32)[:, None], axis=1
    )
    owned = ((expert_ids // EXP_DEV == ep_index) & token_flag[:, None]).reshape(-1)
    slot_ids = (flat_ids % EXP_DEV) * capacity + slot_index
    slot_flag = jnp.any(
        owned[None, :]
        & (slot_ids[None, :] == jnp.arange(EXP_DEV * capacity, dtype=jnp.int32)[:, None]),
        axis=1,
    ).reshape(EXP_DEV, capacity)

    norm_square = jnp.sum(direction_full * direction_full) + 1e-06
    rows = received.astype(jnp.float32)
    products = jnp.einsum("ecm,m->ec", rows, direction_full, precision=lax.Precision.HIGHEST)
    removed = (
        rows - (products / norm_square)[:, :, None] * direction_full[None, None, :]
    ).astype(jnp.bfloat16)
    return jnp.where(slot_flag[:, :, None], removed, received)


def solution(mesh):
    devices = np.asarray(mesh.devices)
    fine = Mesh(devices.reshape(devices.shape[0], RING, RING, 2), ("ctx",) + EP)
    placed = (
        P("ctx", EP),
        P("ctx", EP),
        P("ctx", EP),
        P("ctx", EP),
        P(EP, None),
        P("ctx", None),
        P("ctx"),
        P(EP),
    )
    return jax.shard_map(
        local_body, mesh=fine, in_specs=placed, out_specs=P(EP, "ctx", None), check_vma=False
    )
```

```python
import jax
import jax.numpy as jnp
import numpy as np
from jax import lax
from jax.sharding import Mesh
from jax.sharding import PartitionSpec as P

HEAD = 128
TOP = 2
EXP_DEV = 1
SUB = 256
PAD_ROWS = 8
PARTS = 3
RING = 4
EP = ("x", "y", "core")


def local_step(carried_in, pieces):
    kv_state, offset = carried_in
    query_sub, key_sub, value_sub, decay_sub = pieces
    sub_rows = query_sub.shape[0]
    cumulated = jnp.cumsum(decay_sub, axis=0)
    scores = jnp.einsum("thd,shd->hts", query_sub, key_sub, preferred_element_type=jnp.float32)
    spread = jnp.transpose(cumulated)
    decay_gaps = jnp.minimum(spread[:, :, None] - spread[:, None, :], 0.0)
    causal = (
        jnp.arange(sub_rows, dtype=jnp.int32)[:, None]
        >= jnp.arange(sub_rows, dtype=jnp.int32)[None, :]
    )
    weights = jnp.where(causal[None], scores * jnp.exp(decay_gaps), 0.0).astype(jnp.bfloat16)
    inside = jnp.einsum("hts,shd->thd", weights, value_sub, preferred_element_type=jnp.float32)
    scaled = query_sub.astype(jnp.float32) * jnp.exp(cumulated)[:, :, None]
    carried = jnp.einsum("thd,hde->the", scaled, kv_state, precision=lax.Precision.HIGHEST)
    last_decay = cumulated[-1]
    key_scaled = (
        key_sub.astype(jnp.float32) * jnp.exp(last_decay[None, :] - cumulated)[:, :, None]
    ).astype(jnp.bfloat16)
    update = jnp.einsum("shd,she->hde", key_scaled, value_sub, preferred_element_type=jnp.float32)
    kv_state = jnp.exp(last_decay)[:, None, None] * kv_state + update
    reach_decay = jnp.exp(offset[None, :] + cumulated)
    return ((kv_state, offset + last_decay), (inside + carried, reach_decay))


def normalize(outputs):
    mean_square = jnp.mean(outputs * outputs, axis=-1, keepdims=True)
    return (outputs * lax.rsqrt(mean_square + 1e-06)).astype(jnp.bfloat16)


def combined(left, right):
    right_log = right[:, HEAD:, :]
    gain = jnp.exp(right_log[:, :1, :1])
    state = gain * left[:, :HEAD, :] + right[:, :HEAD, :]
    return jnp.concatenate([state, right_log + left[:, HEAD:, :]], axis=1)


def ring_gathered(blocks, axis):
    def shifted(value, steps):
        return lax.ppermute(value, axis, [(i, (i + steps) % RING) for i in range(RING)])

    half = blocks.shape[-1] // 2
    from_right = shifted(blocks, -1)
    from_left = shifted(blocks, 1)
    far = jnp.concatenate([shifted(blocks[..., :half], 2), shifted(blocks[..., half:], -2)], axis=-1)
    return jnp.concatenate([blocks, from_right, far, from_left], axis=0)


def exclusive_scan(value, axis, count):
    position = lax.axis_index(axis)
    if count == 1:
        return jnp.zeros_like(value)

    def step(current, pairs, chosen, merge):
        arrived = lax.ppermute(current, axis, pairs)
        return arrived, jnp.where(chosen, merge(arrived), current)

    segment = value
    left_raw = None
    distance = 1
    while 4 * distance <= count:
        pairs = [(j - distance, j) for j in range(count) if (j + 1) % (2 * distance) == 0]
        chosen = (position + 1) % (2 * distance) == 0
        arrived, segment = step(segment, pairs, chosen, lambda got, seg=segment: combined(got, seg))
        if left_raw is None:
            left_raw = arrived
        distance *= 2
    distance //= 2
    while distance >= 2:
        pairs = [
            (j, j + distance)
            for j in range(count)
            if (j + 1) % (2 * distance) == 0 and j + distance < count
        ]
        chosen = ((position + 1 - distance) % (2 * distance) == 0) & (position >= 3 * distance - 1)
        _, segment = step(segment, pairs, chosen, lambda got, seg=segment: combined(got, seg))
        distance //= 2
    if left_raw is None:
        left_raw = lax.ppermute(segment, axis, [(j - 1, j) for j in range(1, count, 2)])
    to_even = [(j, j + 1) for j in range(1, count - 1, 2)]
    to_odd = [(j, j + 2) for j in range(1, count - 2, 2)]
    from_odd = lax.ppermute(segment, axis, to_even)
    from_odd_far = lax.ppermute(segment, axis, to_odd)
    odd_result = jnp.where(position >= 3, combined(from_odd_far, left_raw), left_raw)
    result = jnp.where(position % 2 == 1, odd_result, from_odd)
    return jnp.where(position == 0, jnp.zeros_like(value), result)


def split_parts(values, width):
    pieces = []
    rest = values
    for _ in range(PARTS):
        part = lax.reduce_precision(rest, exponent_bits=8, mantissa_bits=7)
        pieces.append(part)
        rest = rest - part
    stacked = jnp.stack(pieces).astype(jnp.bfloat16)
    return jnp.pad(stacked, ((0, PAD_ROWS - PARTS), (0, width - values.shape[0])))


def joined_parts(rows, width, used):
    pieces = rows.astype(jnp.float32).reshape(PARTS, -1, width)[:, :, :used].reshape(PARTS, -1)
    total = pieces[0]
    for part in range(1, PARTS):
        total = total + pieces[part]
    return total


def local_body(queries, key_rows, value_rows, log_decay, out_weight, expert_ids, flagged, direction):
    block_rows = queries.shape[0]
    local_width = queries.shape[1]
    local_heads = local_width // HEAD
    sub_count = block_rows // SUB
    model_cols = out_weight.shape[0]
    ctx_count = lax.axis_size("ctx")
    ctx_index = lax.axis_index("ctx")
    ep_index = lax.axis_index(EP)

    def shaped(operand):
        return operand.reshape(sub_count, SUB, local_heads, HEAD)

    start_state = (
        jnp.zeros((local_heads, HEAD, HEAD), jnp.float32),
        jnp.zeros((local_heads,), jnp.float32),
    )
    scanned = lax.scan(
        local_step,
        start_state,
        (
            shaped(queries),
            shaped(key_rows),
            shaped(value_rows),
            log_decay.reshape(sub_count, SUB, local_heads),
        ),
    )
    local_state, total_decay = scanned[0]
    partial_out, reach_decay = scanned[1]

    packed = jnp.concatenate(
        [local_state, jnp.broadcast_to(total_decay[:, None, None], (local_heads, PAD_ROWS, HEAD))],
        axis=1,
    )
    exclusive = exclusive_scan(packed, "ctx", ctx_count)
    incoming = exclusive[:, :HEAD, :]

    scaled = shaped(queries).astype(jnp.float32) * reach_decay[..., None]
    outputs = partial_out + jnp.einsum(
        "cthd,hde->cthe", scaled, incoming, precision=lax.Precision.HIGHEST
    )
    attended = normalize(outputs).reshape(block_rows, local_width)
    riders = split_parts(direction, local_width)
    block = jnp.concatenate([attended, riders], axis=0)
    near = ring_gathered(block[None], "x")
    near = ring_gathered(near, "y")
    far = lax.ppermute(near, "core", [(0, 1), (1, 0)])

    offsets = jnp.arange(RING, dtype=jnp.int32)
    origin_x = (lax.axis_index("x") + offsets) % RING
    origin_y = (lax.axis_index("y") + offsets) % RING
    near_origin = ((origin_x[None, :] * RING + origin_y[:, None]) * 2).reshape(-1)
    core_index = lax.axis_index("core")
    origin = jnp.concatenate([near_origin + core_index, near_origin + (1 - core_index)])
    slots = origin.shape[0]
    weight_slots = jnp.take(
        out_weight.reshape(model_cols, slots, local_width), origin, axis=1, mode="clip"
    )
    half = near.shape[0]
    projected = lax.dot_general(
        near,
        weight_slots[:, :half],
        (((0, 2), (1, 2)), ((), ())),
        preferred_element_type=jnp.float32,
    ) + lax.dot_general(
        far,
        weight_slots[:, half:],
        (((0, 2), (1, 2)), ((), ())),
        preferred_element_type=jnp.float32,
    )
    projected = projected.astype(jnp.bfloat16)[:block_rows]
    rider_rows = jnp.concatenate(
        [near[:, block_rows : block_rows + PARTS], far[:, block_rows : block_rows + PARTS]], axis=0
    )
    reorder = (origin[None, :] == jnp.arange(slots, dtype=jnp.int32)[:, None]).astype(jnp.bfloat16)
    ordered = jnp.einsum("os,spk->pok", reorder, rider_rows, preferred_element_type=jnp.float32)
    direction_full = joined_parts(ordered.astype(jnp.bfloat16), local_width, model_cols)

    experts_all = lax.axis_size(EP) * EXP_DEV
    capacity = 2 * block_rows * TOP // experts_all
    flat_ids = expert_ids.reshape(-1)
    matches = (flat_ids[:, None] == jnp.arange(experts_all, dtype=jnp.int32)[None, :]).astype(
        jnp.int32
    )
    slot_index = jnp.sum((jnp.cumsum(matches, axis=0) - matches) * matches, axis=1)
    position = (flat_ids * capacity + slot_index).reshape(block_rows, TOP)
    places = jnp.arange(experts_all * capacity, dtype=jnp.int32)[:, None]
    chosen = (position[None, :, 0] == places) | (position[None, :, 1] == places)
    for pick in range(2, TOP):
        chosen = chosen | (position[None, :, pick] == places)
    tile_rows = jnp.einsum(
        "est,tm->esm",
        chosen.astype(jnp.bfloat16).reshape(experts_all, capacity, block_rows),
        projected,
        preferred_element_type=jnp.float32,
    ).astype(jnp.bfloat16)
    received = lax.all_to_all(tile_rows, EP, split_axis=0, concat_axis=2, tiled=True)

    local_flags = flagged - ctx_index * block_rows
    token_flag = jnp.any(
        local_flags[None, :] == jnp.arange(block_rows, dtype=jnp.int32)[:, None], axis=1
    )
    owned = ((expert_ids // EXP_DEV == ep_index) & token_flag[:, None]).reshape(-1)
    slot_ids = (flat_ids % EXP_DEV) * capacity + slot_index
    slot_flag = jnp.any(
        owned[None, :]
        & (slot_ids[None, :] == jnp.arange(EXP_DEV * capacity, dtype=jnp.int32)[:, None]),
        axis=1,
    ).reshape(EXP_DEV, capacity)

    norm_square = jnp.sum(direction_full * direction_full) + 1e-06
    rows = received.astype(jnp.float32)
    products = jnp.einsum("ecm,m->ec", rows, direction_full, precision=lax.Precision.HIGHEST)
    removed = (
        rows - (products / norm_square)[:, :, None] * direction_full[None, None, :]
    ).astype(jnp.bfloat16)
    return jnp.where(slot_flag[:, :, None], removed, received)


def solution(mesh):
    devices = np.asarray(mesh.devices)
    fine = Mesh(devices.reshape(devices.shape[0], RING, RING, 2), ("ctx",) + EP)
    placed = (
        P("ctx", EP),
        P("ctx", EP),
        P("ctx", EP),
        P("ctx", EP),
        P(EP, None),
        P("ctx", None),
        P("ctx"),
        P(EP),
    )
    return jax.shard_map(
        local_body, mesh=fine, in_specs=placed, out_specs=P(EP, "ctx", None), check_vma=False
    )
```

```python
import jax
import jax.numpy as jnp
import numpy as np
from jax import lax
from jax.sharding import Mesh
from jax.sharding import PartitionSpec as P

HEAD = 128
TOP = 2
EXP_DEV = 1
SUB = 256
PAD_ROWS = 8
PARTS = 3
RING = 4
EP = ("x", "y", "core")


def local_step(carried_in, pieces):
    kv_state, offset = carried_in
    query_sub, key_sub, value_sub, decay_sub = pieces
    sub_rows = query_sub.shape[0]
    rows = jnp.arange(sub_rows, dtype=jnp.int32)
    lower = (rows[:, None] >= rows[None, :]).astype(jnp.float32)
    cumulated = jnp.dot(lower, decay_sub, precision=lax.Precision.HIGHEST)
    scores = jnp.einsum("thd,shd->hts", query_sub, key_sub, preferred_element_type=jnp.float32)
    spread = jnp.transpose(cumulated)
    decay_gaps = jnp.minimum(spread[:, :, None] - spread[:, None, :], 0.0)
    causal = (
        jnp.arange(sub_rows, dtype=jnp.int32)[:, None]
        >= jnp.arange(sub_rows, dtype=jnp.int32)[None, :]
    )
    weights = jnp.where(causal[None], scores * jnp.exp(decay_gaps), 0.0).astype(jnp.bfloat16)
    inside = jnp.einsum("hts,shd->thd", weights, value_sub, preferred_element_type=jnp.float32)
    scaled = query_sub.astype(jnp.float32) * jnp.exp(cumulated)[:, :, None]
    carried = jnp.einsum("thd,hde->the", scaled, kv_state, precision=lax.Precision.HIGHEST)
    last_decay = cumulated[-1]
    key_scaled = (
        key_sub.astype(jnp.float32) * jnp.exp(last_decay[None, :] - cumulated)[:, :, None]
    ).astype(jnp.bfloat16)
    update = jnp.einsum("shd,she->hde", key_scaled, value_sub, preferred_element_type=jnp.float32)
    kv_state = jnp.exp(last_decay)[:, None, None] * kv_state + update
    reach_decay = jnp.exp(offset[None, :] + cumulated)
    return ((kv_state, offset + last_decay), (inside + carried, reach_decay))


def normalize(outputs):
    mean_square = jnp.mean(outputs * outputs, axis=-1, keepdims=True)
    return (outputs * lax.rsqrt(mean_square + 1e-06)).astype(jnp.bfloat16)


def combined(left, right):
    right_log = right[:, HEAD:, :]
    gain = jnp.exp(right_log[:, :1, :1])
    state = gain * left[:, :HEAD, :] + right[:, :HEAD, :]
    return jnp.concatenate([state, right_log + left[:, HEAD:, :]], axis=1)


def ring_gathered(blocks, axis):
    def shifted(value, steps):
        return lax.ppermute(value, axis, [(i, (i + steps) % RING) for i in range(RING)])

    half = blocks.shape[-1] // 2
    from_right = shifted(blocks, -1)
    from_left = shifted(blocks, 1)
    far = jnp.concatenate([shifted(blocks[..., :half], 2), shifted(blocks[..., half:], -2)], axis=-1)
    return jnp.concatenate([blocks, from_right, far, from_left], axis=0)


def exclusive_scan(value, axis, count):
    position = lax.axis_index(axis)
    if count == 1:
        return jnp.zeros_like(value)

    def step(current, pairs, chosen, merge):
        arrived = lax.ppermute(current, axis, pairs)
        return arrived, jnp.where(chosen, merge(arrived), current)

    segment = value
    left_raw = None
    distance = 1
    while 4 * distance <= count:
        pairs = [(j - distance, j) for j in range(count) if (j + 1) % (2 * distance) == 0]
        chosen = (position + 1) % (2 * distance) == 0
        arrived, segment = step(segment, pairs, chosen, lambda got, seg=segment: combined(got, seg))
        if left_raw is None:
            left_raw = arrived
        distance *= 2
    distance //= 2
    while distance >= 2:
        pairs = [
            (j, j + distance)
            for j in range(count)
            if (j + 1) % (2 * distance) == 0 and j + distance < count
        ]
        chosen = ((position + 1 - distance) % (2 * distance) == 0) & (position >= 3 * distance - 1)
        _, segment = step(segment, pairs, chosen, lambda got, seg=segment: combined(got, seg))
        distance //= 2
    if left_raw is None:
        left_raw = lax.ppermute(segment, axis, [(j - 1, j) for j in range(1, count, 2)])
    to_even = [(j, j + 1) for j in range(1, count - 1, 2)]
    to_odd = [(j, j + 2) for j in range(1, count - 2, 2)]
    from_odd = lax.ppermute(segment, axis, to_even)
    from_odd_far = lax.ppermute(segment, axis, to_odd)
    odd_result = jnp.where(position >= 3, combined(from_odd_far, left_raw), left_raw)
    result = jnp.where(position % 2 == 1, odd_result, from_odd)
    return jnp.where(position == 0, jnp.zeros_like(value), result)


def split_parts(values, width):
    pieces = []
    rest = values
    for _ in range(PARTS):
        part = lax.reduce_precision(rest, exponent_bits=8, mantissa_bits=7)
        pieces.append(part)
        rest = rest - part
    stacked = jnp.stack(pieces).astype(jnp.bfloat16)
    return jnp.pad(stacked, ((0, PAD_ROWS - PARTS), (0, width - values.shape[0])))


def joined_parts(rows, width, used):
    pieces = rows.astype(jnp.float32).reshape(PARTS, -1, width)[:, :, :used].reshape(PARTS, -1)
    total = pieces[0]
    for part in range(1, PARTS):
        total = total + pieces[part]
    return total


def local_body(queries, key_rows, value_rows, log_decay, out_weight, expert_ids, flagged, direction):
    block_rows = queries.shape[0]
    local_width = queries.shape[1]
    local_heads = local_width // HEAD
    sub_count = block_rows // SUB
    model_cols = out_weight.shape[0]
    ctx_count = lax.axis_size("ctx")
    ctx_index = lax.axis_index("ctx")
    ep_index = lax.axis_index(EP)

    def shaped(operand):
        return operand.reshape(sub_count, SUB, local_heads, HEAD)

    start_state = (
        jnp.zeros((local_heads, HEAD, HEAD), jnp.float32),
        jnp.zeros((local_heads,), jnp.float32),
    )
    scanned = lax.scan(
        local_step,
        start_state,
        (
            shaped(queries),
            shaped(key_rows),
            shaped(value_rows),
            log_decay.reshape(sub_count, SUB, local_heads),
        ),
    )
    local_state, total_decay = scanned[0]
    partial_out, reach_decay = scanned[1]

    packed = jnp.concatenate(
        [local_state, jnp.broadcast_to(total_decay[:, None, None], (local_heads, PAD_ROWS, HEAD))],
        axis=1,
    )
    exclusive = exclusive_scan(packed, "ctx", ctx_count)
    incoming = exclusive[:, :HEAD, :]

    scaled = shaped(queries).astype(jnp.float32) * reach_decay[..., None]
    outputs = partial_out + jnp.einsum(
        "cthd,hde->cthe", scaled, incoming, precision=lax.Precision.HIGHEST
    )
    attended = normalize(outputs).reshape(block_rows, local_width)
    riders = split_parts(direction, local_width)
    block = jnp.concatenate([attended, riders], axis=0)
    near = ring_gathered(block[None], "x")
    near = ring_gathered(near, "y")
    far = lax.ppermute(near, "core", [(0, 1), (1, 0)])

    offsets = jnp.arange(RING, dtype=jnp.int32)
    origin_x = (lax.axis_index("x") + offsets) % RING
    origin_y = (lax.axis_index("y") + offsets) % RING
    near_origin = ((origin_x[None, :] * RING + origin_y[:, None]) * 2).reshape(-1)
    core_index = lax.axis_index("core")
    origin = jnp.concatenate([near_origin + core_index, near_origin + (1 - core_index)])
    slots = origin.shape[0]
    weight_slots = jnp.take(
        out_weight.reshape(model_cols, slots, local_width), origin, axis=1, mode="clip"
    )
    half = near.shape[0]
    projected = lax.dot_general(
        near,
        weight_slots[:, :half],
        (((0, 2), (1, 2)), ((), ())),
        preferred_element_type=jnp.float32,
    ) + lax.dot_general(
        far,
        weight_slots[:, half:],
        (((0, 2), (1, 2)), ((), ())),
        preferred_element_type=jnp.float32,
    )
    projected = projected.astype(jnp.bfloat16)[:block_rows]
    rider_rows = jnp.concatenate(
        [near[:, block_rows : block_rows + PARTS], far[:, block_rows : block_rows + PARTS]], axis=0
    )
    reorder = (origin[None, :] == jnp.arange(slots, dtype=jnp.int32)[:, None]).astype(jnp.bfloat16)
    ordered = jnp.einsum("os,spk->pok", reorder, rider_rows, preferred_element_type=jnp.float32)
    direction_full = joined_parts(ordered.astype(jnp.bfloat16), local_width, model_cols)

    experts_all = lax.axis_size(EP) * EXP_DEV
    capacity = 2 * block_rows * TOP // experts_all
    flat_ids = expert_ids.reshape(-1)
    matches = (flat_ids[:, None] == jnp.arange(experts_all, dtype=jnp.int32)[None, :]).astype(
        jnp.int32
    )
    slot_index = jnp.sum((jnp.cumsum(matches, axis=0) - matches) * matches, axis=1)
    position = (flat_ids * capacity + slot_index).reshape(block_rows, TOP)
    places = jnp.arange(experts_all * capacity, dtype=jnp.int32)[:, None]
    chosen = (position[None, :, 0] == places) | (position[None, :, 1] == places)
    for pick in range(2, TOP):
        chosen = chosen | (position[None, :, pick] == places)
    tile_rows = jnp.dot(
        chosen.astype(jnp.bfloat16), projected, preferred_element_type=jnp.float32
    ).astype(jnp.bfloat16)
    tile_rows = tile_rows.reshape(experts_all, capacity, model_cols)
    received = lax.all_to_all(tile_rows, EP, split_axis=0, concat_axis=2, tiled=True)

    local_flags = flagged - ctx_index * block_rows
    token_flag = jnp.any(
        local_flags[None, :] == jnp.arange(block_rows, dtype=jnp.int32)[:, None], axis=1
    )
    owned = ((expert_ids // EXP_DEV == ep_index) & token_flag[:, None]).reshape(-1)
    slot_ids = (flat_ids % EXP_DEV) * capacity + slot_index
    slot_flag = jnp.any(
        owned[None, :]
        & (slot_ids[None, :] == jnp.arange(EXP_DEV * capacity, dtype=jnp.int32)[:, None]),
        axis=1,
    ).reshape(EXP_DEV, capacity)

    norm_square = jnp.sum(direction_full * direction_full) + 1e-06
    rows = received.astype(jnp.float32)
    products = jnp.einsum("ecm,m->ec", rows, direction_full, precision=lax.Precision.HIGHEST)
    removed = (
        rows - (products / norm_square)[:, :, None] * direction_full[None, None, :]
    ).astype(jnp.bfloat16)
    return jnp.where(slot_flag[:, :, None], removed, received)


def solution(mesh):
    devices = np.asarray(mesh.devices)
    fine = Mesh(devices.reshape(devices.shape[0], RING, RING, 2), ("ctx",) + EP)
    placed = (
        P("ctx", EP),
        P("ctx", EP),
        P("ctx", EP),
        P("ctx", EP),
        P(EP, None),
        P("ctx", None),
        P("ctx"),
        P(EP),
    )
    return jax.shard_map(
        local_body, mesh=fine, in_specs=placed, out_specs=P(EP, "ctx", None), check_vma=False
    )
```

```python
import jax
import jax.numpy as jnp
import numpy as np
from jax import lax
from jax.sharding import Mesh
from jax.sharding import PartitionSpec as P

HEAD = 128
TOP = 2
EXP_DEV = 1
SUB = 256
PAD_ROWS = 8
PARTS = 3
RING = 4
EP = ("x", "y", "core")


def local_step(carried_in, pieces):
    kv_state, offset = carried_in
    query_sub, key_sub, value_sub, decay_sub = pieces
    sub_rows = query_sub.shape[0]
    rows = jnp.arange(sub_rows, dtype=jnp.int32)
    lower = (rows[:, None] >= rows[None, :]).astype(jnp.float32)
    cumulated = jnp.dot(lower, decay_sub, precision=lax.Precision.HIGHEST)
    scores = jnp.einsum("thd,shd->hts", query_sub, key_sub, preferred_element_type=jnp.float32)
    spread = jnp.transpose(cumulated)
    decay_gaps = jnp.minimum(spread[:, :, None] - spread[:, None, :], 0.0)
    causal = (
        jnp.arange(sub_rows, dtype=jnp.int32)[:, None]
        >= jnp.arange(sub_rows, dtype=jnp.int32)[None, :]
    )
    weights = jnp.where(causal[None], scores * jnp.exp(decay_gaps), 0.0).astype(jnp.bfloat16)
    inside = jnp.einsum("hts,shd->thd", weights, value_sub, preferred_element_type=jnp.float32)
    scaled = query_sub.astype(jnp.float32) * jnp.exp(cumulated)[:, :, None]
    carried = jnp.einsum("thd,hde->the", scaled, kv_state, precision=lax.Precision.HIGHEST)
    last_decay = cumulated[-1]
    key_scaled = (
        key_sub.astype(jnp.float32) * jnp.exp(last_decay[None, :] - cumulated)[:, :, None]
    ).astype(jnp.bfloat16)
    update = jnp.einsum("shd,she->hde", key_scaled, value_sub, preferred_element_type=jnp.float32)
    kv_state = jnp.exp(last_decay)[:, None, None] * kv_state + update
    reach_decay = jnp.exp(offset[None, :] + cumulated)
    return ((kv_state, offset + last_decay), (inside + carried, reach_decay))


def normalize(outputs):
    mean_square = jnp.mean(outputs * outputs, axis=-1, keepdims=True)
    return (outputs * lax.rsqrt(mean_square + 1e-06)).astype(jnp.bfloat16)


def combined(left, right):
    right_log = right[:, HEAD:, :]
    gain = jnp.exp(right_log[:, :1, :1])
    state = gain * left[:, :HEAD, :] + right[:, :HEAD, :]
    return jnp.concatenate([state, right_log + left[:, HEAD:, :]], axis=1)


def ring_gathered(blocks, axis):
    def shifted(value, steps):
        return lax.ppermute(value, axis, [(i, (i + steps) % RING) for i in range(RING)])

    half = blocks.shape[-1] // 2
    from_right = shifted(blocks, -1)
    from_left = shifted(blocks, 1)
    far = jnp.concatenate([shifted(blocks[..., :half], 2), shifted(blocks[..., half:], -2)], axis=-1)
    return jnp.concatenate([blocks, from_right, far, from_left], axis=0)


def exclusive_scan(value, axis, count):
    position = lax.axis_index(axis)
    if count == 1:
        return jnp.zeros_like(value)

    def step(current, pairs, chosen, merge):
        arrived = lax.ppermute(current, axis, pairs)
        return arrived, jnp.where(chosen, merge(arrived), current)

    segment = value
    left_raw = None
    distance = 1
    while 4 * distance <= count:
        pairs = [(j - distance, j) for j in range(count) if (j + 1) % (2 * distance) == 0]
        chosen = (position + 1) % (2 * distance) == 0
        arrived, segment = step(segment, pairs, chosen, lambda got, seg=segment: combined(got, seg))
        if left_raw is None:
            left_raw = arrived
        distance *= 2
    distance //= 2
    while distance >= 2:
        pairs = [
            (j, j + distance)
            for j in range(count)
            if (j + 1) % (2 * distance) == 0 and j + distance < count
        ]
        chosen = ((position + 1 - distance) % (2 * distance) == 0) & (position >= 3 * distance - 1)
        _, segment = step(segment, pairs, chosen, lambda got, seg=segment: combined(got, seg))
        distance //= 2
    if left_raw is None:
        left_raw = lax.ppermute(segment, axis, [(j - 1, j) for j in range(1, count, 2)])
    to_even = [(j, j + 1) for j in range(1, count - 1, 2)]
    to_odd = [(j, j + 2) for j in range(1, count - 2, 2)]
    from_odd = lax.ppermute(segment, axis, to_even)
    from_odd_far = lax.ppermute(segment, axis, to_odd)
    odd_result = jnp.where(position >= 3, combined(from_odd_far, left_raw), left_raw)
    return jnp.where(position % 2 == 1, odd_result, from_odd)


def split_parts(values, width):
    pieces = []
    rest = values
    for _ in range(PARTS):
        part = lax.reduce_precision(rest, exponent_bits=8, mantissa_bits=7)
        pieces.append(part)
        rest = rest - part
    stacked = jnp.stack(pieces).astype(jnp.bfloat16)
    return jnp.pad(stacked, ((0, PAD_ROWS - PARTS), (0, width - values.shape[0])))


def joined_parts(rows, width, used):
    pieces = rows.astype(jnp.float32).reshape(PARTS, -1, width)[:, :, :used].reshape(PARTS, -1)
    total = pieces[0]
    for part in range(1, PARTS):
        total = total + pieces[part]
    return total


def local_body(queries, key_rows, value_rows, log_decay, out_weight, expert_ids, flagged, direction):
    block_rows = queries.shape[0]
    local_width = queries.shape[1]
    local_heads = local_width // HEAD
    sub_count = block_rows // SUB
    model_cols = out_weight.shape[0]
    ctx_count = lax.axis_size("ctx")
    ctx_index = lax.axis_index("ctx")
    ep_index = lax.axis_index(EP)

    def shaped(operand):
        return operand.reshape(sub_count, SUB, local_heads, HEAD)

    start_state = (
        jnp.zeros((local_heads, HEAD, HEAD), jnp.float32),
        jnp.zeros((local_heads,), jnp.float32),
    )
    scanned = lax.scan(
        local_step,
        start_state,
        (
            shaped(queries),
            shaped(key_rows),
            shaped(value_rows),
            log_decay.reshape(sub_count, SUB, local_heads),
        ),
    )
    local_state, total_decay = scanned[0]
    partial_out, reach_decay = scanned[1]

    packed = jnp.concatenate(
        [local_state, jnp.broadcast_to(total_decay[:, None, None], (local_heads, PAD_ROWS, HEAD))],
        axis=1,
    )
    exclusive = exclusive_scan(packed, "ctx", ctx_count)
    incoming = exclusive[:, :HEAD, :]

    scaled = shaped(queries).astype(jnp.float32) * reach_decay[..., None]
    outputs = partial_out + jnp.einsum(
        "cthd,hde->cthe", scaled, incoming, precision=lax.Precision.HIGHEST
    )
    attended = normalize(outputs).reshape(block_rows, local_width)
    riders = split_parts(direction, local_width)
    block = jnp.concatenate([attended, riders], axis=0)
    near = ring_gathered(block[None], "x")
    near = ring_gathered(near, "y")
    far = lax.ppermute(near, "core", [(0, 1), (1, 0)])

    offsets = jnp.arange(RING, dtype=jnp.int32)
    origin_x = (lax.axis_index("x") + offsets) % RING
    origin_y = (lax.axis_index("y") + offsets) % RING
    near_origin = ((origin_x[None, :] * RING + origin_y[:, None]) * 2).reshape(-1)
    core_index = lax.axis_index("core")
    origin = jnp.concatenate([near_origin + core_index, near_origin + (1 - core_index)])
    slots = origin.shape[0]
    weight_slots = jnp.take(
        out_weight.reshape(model_cols, slots, local_width), origin, axis=1, mode="clip"
    )
    half = near.shape[0]
    projected = lax.dot_general(
        near,
        weight_slots[:, :half],
        (((0, 2), (1, 2)), ((), ())),
        preferred_element_type=jnp.float32,
    ) + lax.dot_general(
        far,
        weight_slots[:, half:],
        (((0, 2), (1, 2)), ((), ())),
        preferred_element_type=jnp.float32,
    )
    projected = projected.astype(jnp.bfloat16)[:block_rows]
    rider_rows = jnp.concatenate(
        [near[:, block_rows : block_rows + PARTS], far[:, block_rows : block_rows + PARTS]], axis=0
    )
    reorder = (origin[None, :] == jnp.arange(slots, dtype=jnp.int32)[:, None]).astype(jnp.bfloat16)
    ordered = jnp.einsum("os,spk->pok", reorder, rider_rows, preferred_element_type=jnp.float32)
    direction_full = joined_parts(ordered.astype(jnp.bfloat16), local_width, model_cols)

    experts_all = lax.axis_size(EP) * EXP_DEV
    capacity = 2 * block_rows * TOP // experts_all
    flat_ids = expert_ids.reshape(-1)
    matches = (flat_ids[:, None] == jnp.arange(experts_all, dtype=jnp.int32)[None, :]).astype(
        jnp.int32
    )
    slot_index = jnp.sum((jnp.cumsum(matches, axis=0) - matches) * matches, axis=1)
    position = (flat_ids * capacity + slot_index).reshape(block_rows, TOP)
    places = jnp.arange(experts_all * capacity, dtype=jnp.int32)[:, None]
    chosen = (position[None, :, 0] == places) | (position[None, :, 1] == places)
    for pick in range(2, TOP):
        chosen = chosen | (position[None, :, pick] == places)
    tile_rows = jnp.einsum(
        "est,tm->esm",
        chosen.astype(jnp.bfloat16).reshape(experts_all, capacity, block_rows),
        projected,
        preferred_element_type=jnp.float32,
    ).astype(jnp.bfloat16)
    received = lax.all_to_all(tile_rows, EP, split_axis=0, concat_axis=2, tiled=True)

    local_flags = flagged - ctx_index * block_rows
    token_flag = jnp.any(
        local_flags[None, :] == jnp.arange(block_rows, dtype=jnp.int32)[:, None], axis=1
    )
    owned = ((expert_ids // EXP_DEV == ep_index) & token_flag[:, None]).reshape(-1)
    slot_ids = (flat_ids % EXP_DEV) * capacity + slot_index
    slot_flag = jnp.any(
        owned[None, :]
        & (slot_ids[None, :] == jnp.arange(EXP_DEV * capacity, dtype=jnp.int32)[:, None]),
        axis=1,
    ).reshape(EXP_DEV, capacity)

    norm_square = jnp.sum(direction_full * direction_full) + 1e-06
    rows = received.astype(jnp.float32)
    products = jnp.einsum("ecm,m->ec", rows, direction_full, precision=lax.Precision.HIGHEST)
    removed = (
        rows - (products / norm_square)[:, :, None] * direction_full[None, None, :]
    ).astype(jnp.bfloat16)
    return jnp.where(slot_flag[:, :, None], removed, received)


def solution(mesh):
    devices = np.asarray(mesh.devices)
    fine = Mesh(devices.reshape(devices.shape[0], RING, RING, 2), ("ctx",) + EP)
    placed = (
        P("ctx", EP),
        P("ctx", EP),
        P("ctx", EP),
        P("ctx", EP),
        P(EP, None),
        P("ctx", None),
        P("ctx"),
        P(EP),
    )
    return jax.shard_map(
        local_body, mesh=fine, in_specs=placed, out_specs=P(EP, "ctx", None), check_vma=False
    )
```
